32 devices in a mesh: grp: 2 (over y), seq: 4 (over z), head: 2 (over x), sub: 2 (over core).
Axes of the slice: x: 2, y: 2, z: 4, core: 2. Of those that a mesh axis runs over, the one named last changes fastest.
Arguments:
- queries: bfloat16 [4096, 64, 128], P(('grp', 'seq'), ('head', 'sub')), parts along dimension 0, may hold values from -6 to 6
- key_rows: bfloat16 [4096, 64, 128], P(('grp', 'seq'), ('head', 'sub')), parts along dimension 0, may hold values from -6 to 6
- value_rows: bfloat16 [4096, 64, 128], P(('grp', 'seq'), ('head', 'sub')), parts along dimension 0, may hold values from -6 to 6
- out_adjoint: bfloat16 [4096, 64, 128], P(('grp', 'seq'), ('head', 'sub')), parts along dimension 0, may hold values from -6 to 6
Outputs:
- attended: bfloat16 [4096, 64, 128], P(('grp', 'seq'), ('head', 'sub')), parts along dimension 0
- query_grad: bfloat16 [4096, 64, 128], P(('grp', 'seq', 'head', 'sub')), parts along dimension 0
- key_grad: bfloat16 [4096, 64, 128], P(('grp', 'seq', 'head', 'sub')), parts along dimension 0
- value_grad: bfloat16 [4096, 64, 128], P(('grp', 'seq', 'head', 'sub')), parts along dimension 0
The draws below stay inside these ranges and needn't reach their ends.
There are 2 independent parts, one for each index of `grp`. The reference program is written for one: setup_inputs(seed, part) draws one part's arguments, and reference() takes and returns one part's arrays. A program takes and returns all parts, laid end to end along the dimension named above; each array names one. Nothing has to cross between parts.
All inputs are finite; a program needn't handle non-finite values.
Results may differ from the reference program's by a relative error of at most 0.0058.
Values may be sent and summed in bfloat16 or wider, within the bound.
No kernel may reach another device: no remote copies, remote signals or barrier semaphores. Data moves between devices by JAX's collectives and lax.ppermute only.
A program may use at most 128 MiB of HBM per device.

```python
import jax
import jax.numpy as jnp
from jax import lax

HEADS = 64
HEAD_DIM = 128
SPAN = 64
TOKENS = 2048


def shard_levels(rng, dims, pieces, low, top_value):
    level = 1.0
    for dim, blocks in pieces:
        draws = jax.random.uniform(jax.random.fold_in(jax.random.fold_in(rng, 6), dim), (blocks,), jnp.float32, low / len(pieces), top_value / len(pieces))
        level = level * jnp.repeat(jnp.exp(draws), dims[dim] // blocks).reshape((-1,) + (1,) * (len(dims) - 1 - dim))
    return level


def bell_draw(rng, extent, width, reach, pieces=(), kind=jnp.bfloat16):
    level = shard_levels(rng, extent, pieces, -0.22, 0.18) if pieces else 1.0
    entries = jax.random.normal(rng, extent, jnp.float32) * width * level
    return jnp.minimum(jnp.maximum(entries, -reach), reach).astype(kind)


def setup_inputs(seed: int = 0, part: int = 0) -> dict:
    keys = jax.random.split(jax.random.key(seed), 5)
    part_splits = jax.random.split(jax.random.fold_in(keys[4], part), 5)
    return {
        "queries": bell_draw(part_splits[0], (TOKENS, HEADS, HEAD_DIM), 1.0, 6.0, ((0, 4), (1, 4))),
        "key_rows": bell_draw(part_splits[1], (TOKENS, HEADS, HEAD_DIM), 1.0, 6.0, ((0, 4), (1, 4))),
        "value_rows": bell_draw(part_splits[2], (TOKENS, HEADS, HEAD_DIM), 1.0, 6.0, ((0, 4), (1, 4))),
        "out_adjoint": bell_draw(part_splits[3], (TOKENS, HEADS, HEAD_DIM), 1.0, 6.0, ((0, 4), (1, 4))),
    }


def one_head(operands):
    queries, key_rows, value_rows, out_adjoint = operands
    blocks = TOKENS // SPAN
    position = jnp.arange(TOKENS, dtype=jnp.int32)
    factor = lax.rsqrt(jnp.float32(HEAD_DIM) * (position + 1).astype(jnp.float32))
    scaled = (queries.astype(jnp.float32) * factor[:, None]).astype(jnp.bfloat16)
    qsc = scaled.reshape(blocks, SPAN, HEAD_DIM).astype(jnp.float32)
    kch = key_rows.reshape(blocks, SPAN, HEAD_DIM).astype(jnp.float32)
    vch = value_rows.reshape(blocks, SPAN, HEAD_DIM).astype(jnp.float32)
    dch = out_adjoint.reshape(blocks, SPAN, HEAD_DIM).astype(jnp.float32)
    kv_block = jnp.einsum('ncd,nce->nde', kch, vch)
    state = jnp.cumsum(kv_block, 0) - kv_block
    state_low = state.astype(jnp.bfloat16).astype(jnp.float32)
    adj_block = jnp.einsum('nce,ncd->ned', dch, qsc)
    suffix = jnp.cumsum(adj_block[::-1], 0)[::-1] - adj_block
    suffix_low = suffix.astype(jnp.bfloat16).astype(jnp.float32)
    row = jnp.arange(SPAN, dtype=jnp.int32)
    causal = row[:, None] >= row[None, :]
    scores = jnp.where(causal[None], jnp.einsum('ncd,nsd->ncs', qsc, kch), 0.0)
    scores = scores.astype(jnp.bfloat16).astype(jnp.float32)
    attended = jnp.einsum('ncd,nde->nce', qsc, state_low) + jnp.einsum('ncs,nse->nce', scores, vch)
    adj_scores = jnp.where(causal[None], jnp.einsum('nce,nse->ncs', dch, vch), 0.0)
    adj_scores = adj_scores.astype(jnp.bfloat16).astype(jnp.float32)
    query_grad = (jnp.einsum('nce,nde->ncd', dch, state_low) + jnp.einsum('ncs,nsd->ncd', adj_scores, kch)) * factor.reshape(blocks, SPAN, 1)
    key_grad = jnp.einsum('nse,ned->nsd', vch, suffix_low) + jnp.einsum('ncs,ncd->nsd', adj_scores, qsc)
    value_grad = jnp.einsum('nsd,ned->nse', kch, suffix_low) + jnp.einsum('ncs,nce->nse', scores, dch)
    shape = (TOKENS, HEAD_DIM)
    return (attended.reshape(shape).astype(jnp.bfloat16), query_grad.reshape(shape).astype(jnp.bfloat16), key_grad.reshape(shape).astype(jnp.bfloat16), value_grad.reshape(shape).astype(jnp.bfloat16))

def reference(queries, key_rows, value_rows, out_adjoint):
    moved = (jnp.transpose(queries, (1, 0, 2)), jnp.transpose(key_rows, (1, 0, 2)), jnp.transpose(value_rows, (1, 0, 2)), jnp.transpose(out_adjoint, (1, 0, 2)))
    results = lax.map(one_head, moved)
    attended, query_grad, key_grad, value_grad = [jnp.transpose(r, (1, 0, 2)) for r in results]
    return (attended, query_grad, key_grad, value_grad)
```

```python
import jax
import jax.numpy as jnp
from jax import lax
from jax.sharding import PartitionSpec as P

SPAN = 64
PIECES = 4
SEQ = 1


def exclusive_scan(total, axis, count, reverse, pieces):
    outs = []
    for chunk in jnp.split(total, pieces, axis=0):
        carried = jnp.zeros_like(chunk)
        acc = jnp.zeros_like(chunk)
        for hop in range(count - 1):
            pair = (count - 1 - hop, count - 2 - hop) if reverse else (hop, hop + 1)
            got = lax.ppermute(carried + chunk, axis, perm=[pair])
            acc = acc + got
            carried = got
        outs.append(acc)
    return jnp.concatenate(outs, 0)


def per_device(queries, key_rows, value_rows, out_adjoint):
    tok_dev, heads_dev, head_dim = queries.shape
    span = SPAN
    blocks = tok_dev // span
    offset = lax.axis_index("seq") * tok_dev
    position = offset + jnp.arange(tok_dev, dtype=jnp.int32)
    factor = lax.rsqrt(jnp.float32(head_dim) * (position + 1).astype(jnp.float32))
    scaled = (queries.astype(jnp.float32) * factor[:, None, None]).astype(jnp.bfloat16)
    qsc = scaled.reshape(blocks, span, heads_dev, head_dim)
    kch = key_rows.reshape(blocks, span, heads_dev, head_dim)
    vch = value_rows.reshape(blocks, span, heads_dev, head_dim)
    dch = out_adjoint.reshape(blocks, span, heads_dev, head_dim)
    kv_block = jnp.einsum("nchd,nche->nhde", kch, vch, preferred_element_type=jnp.float32)
    adj_block = jnp.einsum("nche,nchd->nhed", dch, qsc, preferred_element_type=jnp.float32)
    kv_total = jnp.sum(kv_block, 0)
    adj_total = jnp.sum(adj_block, 0)
    before = exclusive_scan(kv_total, "seq", SEQ, False, PIECES)
    after = exclusive_scan(adj_total, "seq", SEQ, True, PIECES)
    state = before[None] + jnp.cumsum(kv_block, 0) - kv_block
    suffix = after[None] + jnp.cumsum(adj_block[::-1], 0)[::-1] - adj_block
    state_low = state.astype(jnp.bfloat16)
    suffix_low = suffix.astype(jnp.bfloat16)
    row = jnp.arange(span, dtype=jnp.int32)
    causal = (row[:, None] >= row[None, :])[None, None]
    scores = jnp.where(
        causal, jnp.einsum("nchd,nshd->nhcs", qsc, kch, preferred_element_type=jnp.float32), 0.0
    ).astype(jnp.bfloat16)
    attended = jnp.einsum(
        "nchd,nhde->nche", qsc, state_low, preferred_element_type=jnp.float32
    ) + jnp.einsum("nhcs,nshe->nche", scores, vch, preferred_element_type=jnp.float32)
    adj_scores = jnp.where(
        causal, jnp.einsum("nche,nshe->nhcs", dch, vch, preferred_element_type=jnp.float32), 0.0
    ).astype(jnp.bfloat16)
    query_grad = (
        jnp.einsum("nche,nhde->nchd", dch, state_low, preferred_element_type=jnp.float32)
        + jnp.einsum("nhcs,nshd->nchd", adj_scores, kch, preferred_element_type=jnp.float32)
    ) * factor.reshape(blocks, span, 1, 1)
    key_grad = jnp.einsum(
        "nshe,nhed->nshd", vch, suffix_low, preferred_element_type=jnp.float32
    ) + jnp.einsum("nhcs,nchd->nshd", adj_scores, qsc, preferred_element_type=jnp.float32)
    value_grad = jnp.einsum(
        "nshd,nhed->nshe", kch, suffix_low, preferred_element_type=jnp.float32
    ) + jnp.einsum("nhcs,nche->nshe", scores, dch, preferred_element_type=jnp.float32)
    shape = (tok_dev, heads_dev, head_dim)
    attended = attended.reshape(shape).astype(jnp.bfloat16)
    query_grad = query_grad.reshape(shape).astype(jnp.bfloat16)
    key_grad = key_grad.reshape(shape).astype(jnp.bfloat16)
    value_grad = value_grad.reshape(shape).astype(jnp.bfloat16)
    query_out, key_out, value_out = (
        lax.all_to_all(query_grad, ("head", "sub"), split_axis=0, concat_axis=1, tiled=True),
        lax.all_to_all(key_grad, ("head", "sub"), split_axis=0, concat_axis=1, tiled=True),
        lax.all_to_all(value_grad, ("head", "sub"), split_axis=0, concat_axis=1, tiled=True),
    )
    return (attended, query_out, key_out, value_out)


def solution(mesh):
    global SEQ
    SEQ = mesh.shape["seq"]
    in_specs = (
        P(("grp", "seq"), ("head", "sub"), None),
        P(("grp", "seq"), ("head", "sub"), None),
        P(("grp", "seq"), ("head", "sub"), None),
        P(("grp", "seq"), ("head", "sub"), None),
    )
    out_specs = (
        P(("grp", "seq"), ("head", "sub"), None),
        P(("grp", "seq", "head", "sub"), None, None),
        P(("grp", "seq", "head", "sub"), None, None),
        P(("grp", "seq", "head", "sub"), None, None),
    )
    return jax.shard_map(
        per_device, mesh=mesh, in_specs=in_specs, out_specs=out_specs, check_vma=False
    )
```

```python
import jax
import jax.numpy as jnp
from jax import lax
from jax.sharding import PartitionSpec as P

SPAN = 64
GROUPS = 4


def exclusive_scan(total, axis, count, reverse):
    carried = jnp.zeros_like(total)
    acc = jnp.zeros_like(total)
    for hop in range(count - 1):
        pair = (count - 1 - hop, count - 2 - hop) if reverse else (hop, hop + 1)
        got = lax.ppermute(carried + total, axis, perm=[pair])
        acc = acc + got
        carried = got
    return acc


def head_group(qsc, kch, vch, dch, factor, seq_count):
    blocks, span, heads, head_dim = qsc.shape
    kv_block = jnp.einsum("nchd,nche->nhde", kch, vch, preferred_element_type=jnp.float32)
    adj_block = jnp.einsum("nche,nchd->nhed", dch, qsc, preferred_element_type=jnp.float32)
    before = exclusive_scan(jnp.sum(kv_block, 0), "seq", seq_count, False)
    after = exclusive_scan(jnp.sum(adj_block, 0), "seq", seq_count, True)
    state = before[None] + jnp.cumsum(kv_block, 0) - kv_block
    suffix = after[None] + jnp.cumsum(adj_block[::-1], 0)[::-1] - adj_block
    state_low = state.astype(jnp.bfloat16)
    suffix_low = suffix.astype(jnp.bfloat16)
    row = jnp.arange(span, dtype=jnp.int32)
    causal = (row[:, None] >= row[None, :])[None, None]
    scores = jnp.where(
        causal, jnp.einsum("nchd,nshd->nhcs", qsc, kch, preferred_element_type=jnp.float32), 0.0
    ).astype(jnp.bfloat16)
    attended = jnp.einsum(
        "nchd,nhde->nche", qsc, state_low, preferred_element_type=jnp.float32
    ) + jnp.einsum("nhcs,nshe->nche", scores, vch, preferred_element_type=jnp.float32)
    adj_scores = jnp.where(
        causal, jnp.einsum("nche,nshe->nhcs", dch, vch, preferred_element_type=jnp.float32), 0.0
    ).astype(jnp.bfloat16)
    query_grad = (
        jnp.einsum("nche,nhde->nchd", dch, state_low, preferred_element_type=jnp.float32)
        + jnp.einsum("nhcs,nshd->nchd", adj_scores, kch, preferred_element_type=jnp.float32)
    ) * factor.reshape(blocks, span, 1, 1)
    key_grad = jnp.einsum(
        "nshe,nhed->nshd", vch, suffix_low, preferred_element_type=jnp.float32
    ) + jnp.einsum("nhcs,nchd->nshd", adj_scores, qsc, preferred_element_type=jnp.float32)
    value_grad = jnp.einsum(
        "nshd,nhed->nshe", kch, suffix_low, preferred_element_type=jnp.float32
    ) + jnp.einsum("nhcs,nche->nshe", scores, dch, preferred_element_type=jnp.float32)
    shape = (blocks * span, heads, head_dim)
    grads = jnp.concatenate(
        [g.reshape(shape).astype(jnp.bfloat16) for g in (query_grad, key_grad, value_grad)], 1
    )
    grads = lax.all_to_all(grads, ("head", "sub"), split_axis=0, concat_axis=1, tiled=True)
    return attended.reshape(shape).astype(jnp.bfloat16), grads


def per_device(queries, key_rows, value_rows, out_adjoint, seq_count):
    tok_dev, heads_dev, head_dim = queries.shape
    span = SPAN
    blocks = tok_dev // span
    groups = GROUPS if heads_dev % GROUPS == 0 else 1
    width = heads_dev // groups
    offset = lax.axis_index("seq") * tok_dev
    position = offset + jnp.arange(tok_dev, dtype=jnp.int32)
    factor = lax.rsqrt(jnp.float32(head_dim) * (position + 1).astype(jnp.float32))
    scaled = (queries.astype(jnp.float32) * factor[:, None, None]).astype(jnp.bfloat16)
    attended, grads = [], []
    for g in range(groups):
        part = lambda x: x[:, g * width:(g + 1) * width].reshape(blocks, span, width, head_dim)
        a, gr = head_group(
            part(scaled), part(key_rows), part(value_rows), part(out_adjoint), factor, seq_count
        )
        attended.append(a)
        grads.append(gr.reshape(gr.shape[0], -1, 3, width, head_dim))
    attended = jnp.concatenate(attended, 1)
    stacked = jnp.stack(grads, 3)
    outs = tuple(stacked[:, :, i].reshape(stacked.shape[0], -1, head_dim) for i in range(3))
    return (attended,) + outs


def solution(mesh):
    seq_count = mesh.shape["seq"]
    in_specs = (
        P(("grp", "seq"), ("head", "sub"), None),
        P(("grp", "seq"), ("head", "sub"), None),
        P(("grp", "seq"), ("head", "sub"), None),
        P(("grp", "seq"), ("head", "sub"), None),
    )
    out_specs = (
        P(("grp", "seq"), ("head", "sub"), None),
        P(("grp", "seq", "head", "sub"), None, None),
        P(("grp", "seq", "head", "sub"), None, None),
        P(("grp", "seq", "head", "sub"), None, None),
    )
    return jax.shard_map(
        lambda *a: per_device(*a, seq_count),
        mesh=mesh, in_specs=in_specs, out_specs=out_specs, check_vma=False,
    )
```

```python
import functools

import jax
import jax.numpy as jnp
from jax import lax
from jax.experimental import pallas as pl
from jax.experimental.pallas import tpu as pltpu
from jax.sharding import PartitionSpec as P

SPAN = 64
F32 = jnp.float32
BF16 = jnp.bfloat16


def dot_nn(a, b):
    return jnp.dot(a, b, preferred_element_type=F32)


def dot_nt(a, b):
    return lax.dot_general(a, b, (((1,), (1,)), ((), ())), preferred_element_type=F32)


def dot_tn(a, b):
    return lax.dot_general(a, b, (((0,), (0,)), ((), ())), preferred_element_type=F32)


def totals_kernel(heads, q_ref, k_ref, v_ref, d_ref, f_ref, kv_ref, adj_ref):
    @pl.when(pl.program_id(0) == 0)
    def _():
        kv_ref[...] = jnp.zeros_like(kv_ref)
        adj_ref[...] = jnp.zeros_like(adj_ref)

    factor = f_ref[...]
    for h in range(heads):
        qsc = (q_ref[:, h, :].astype(F32) * factor).astype(BF16)
        kv_ref[h] += dot_tn(k_ref[:, h, :], v_ref[:, h, :])
        adj_ref[h] += dot_tn(d_ref[:, h, :], qsc)


def main_kernel(heads, q_ref, k_ref, v_ref, d_ref, f_ref, before_ref, rest_ref,
                a_ref, qg_ref, kg_ref, vg_ref, state, suffix):
    @pl.when(pl.program_id(0) == 0)
    def _():
        state[...] = before_ref[...]
        suffix[...] = rest_ref[...]

    factor = f_ref[...]
    span = factor.shape[0]
    row = lax.broadcasted_iota(jnp.int32, (span, span), 0)
    col = lax.broadcasted_iota(jnp.int32, (span, span), 1)
    causal = row >= col
    for h in range(heads):
        q = q_ref[:, h, :]
        k = k_ref[:, h, :]
        v = v_ref[:, h, :]
        d = d_ref[:, h, :]
        qsc = (q.astype(F32) * factor).astype(BF16)
        prev = state[h]
        state_low = prev.astype(BF16)
        state[h] = prev + dot_tn(k, v)
        rest = suffix[h] - dot_tn(d, qsc)
        suffix[h] = rest
        suffix_low = rest.astype(BF16)
        scores = jnp.where(causal, dot_nt(qsc, k), 0.0).astype(BF16)
        adj_scores = jnp.where(causal, dot_nt(d, v), 0.0).astype(BF16)
        a_ref[:, h, :] = (dot_nn(qsc, state_low) + dot_nn(scores, v)).astype(a_ref.dtype)
        qg_ref[:, h, :] = ((dot_nt(d, state_low) + dot_nn(adj_scores, k)) * factor).astype(qg_ref.dtype)
        kg_ref[:, h, :] = (dot_nn(v, suffix_low) + dot_tn(adj_scores, qsc)).astype(kg_ref.dtype)
        vg_ref[:, h, :] = (dot_nt(k, suffix_low) + dot_tn(scores, d)).astype(vg_ref.dtype)


def exclusive_scan(total, axis, count, reverse):
    carried = jnp.zeros_like(total)
    acc = jnp.zeros_like(total)
    for hop in range(count - 1):
        pair = (count - 1 - hop, count - 2 - hop) if reverse else (hop, hop + 1)
        got = lax.ppermute(carried + total, axis, perm=[pair])
        acc = acc + got
        carried = got
    return acc


def per_device(queries, key_rows, value_rows, out_adjoint, seq_count):
    tok_dev, heads, head_dim = queries.shape
    span = SPAN
    blocks = tok_dev // span
    offset = lax.axis_index("seq") * tok_dev
    position = offset + jnp.arange(tok_dev, dtype=jnp.int32)
    factor = lax.rsqrt(jnp.float32(head_dim) * (position + 1).astype(jnp.float32))[:, None]

    tile = pl.BlockSpec((span, heads, head_dim), lambda c: (c, 0, 0))
    fac = pl.BlockSpec((span, 1), lambda c: (c, 0))
    whole = pl.BlockSpec((heads, head_dim, head_dim), lambda c: (0, 0, 0))
    state_shape = jax.ShapeDtypeStruct((heads, head_dim, head_dim), F32)
    kv_total, adj_total = pl.pallas_call(
        functools.partial(totals_kernel, heads),
        grid=(blocks,),
        in_specs=[tile, tile, tile, tile, fac],
        out_specs=[whole, whole],
        out_shape=[state_shape, state_shape],
        compiler_params=pltpu.CompilerParams(dimension_semantics=("arbitrary",)),
    )(queries, key_rows, value_rows, out_adjoint, factor)

    before = exclusive_scan(kv_total, "seq", seq_count, False)
    after = exclusive_scan(adj_total, "seq", seq_count, True)
    rest = after + adj_total

    out_tile = jax.ShapeDtypeStruct((tok_dev, heads, head_dim), BF16)
    attended, query_grad, key_grad, value_grad = pl.pallas_call(
        functools.partial(main_kernel, heads),
        grid=(blocks,),
        in_specs=[tile, tile, tile, tile, fac, whole, whole],
        out_specs=[tile, tile, tile, tile],
        out_shape=[out_tile] * 4,
        scratch_shapes=[pltpu.VMEM((heads, head_dim, head_dim), F32)] * 2,
        compiler_params=pltpu.CompilerParams(dimension_semantics=("arbitrary",)),
    )(queries, key_rows, value_rows, out_adjoint, factor, before, rest)

    outs = tuple(
        lax.all_to_all(g, ("head", "sub"), split_axis=0, concat_axis=1, tiled=True)
        for g in (query_grad, key_grad, value_grad)
    )
    return (attended,) + outs


def solution(mesh):
    seq_count = mesh.shape["seq"]
    spec_in = P(("grp", "seq"), ("head", "sub"), None)
    spec_grad = P(("grp", "seq", "head", "sub"), None, None)
    return jax.shard_map(
        lambda *a: per_device(*a, seq_count),
        mesh=mesh,
        in_specs=(spec_in,) * 4,
        out_specs=(spec_in, spec_grad, spec_grad, spec_grad),
        check_vma=False,
    )
```

```python
import functools

import jax
import jax.numpy as jnp
from jax import lax
from jax.experimental import pallas as pl
from jax.experimental.pallas import tpu as pltpu
from jax.sharding import PartitionSpec as P

SPAN = 64
F32 = jnp.float32
BF16 = jnp.bfloat16


def dot_nn(a, b):
    return jnp.dot(a, b, preferred_element_type=F32)


def dot_nt(a, b):
    return lax.dot_general(a, b, (((1,), (1,)), ((), ())), preferred_element_type=F32)


def dot_tn(a, b):
    return lax.dot_general(a, b, (((0,), (0,)), ((), ())), preferred_element_type=F32)


def totals_kernel(heads, q_ref, k_ref, v_ref, d_ref, f_ref, kv_ref, adj_ref):
    @pl.when(pl.program_id(0) == 0)
    def _():
        kv_ref[...] = jnp.zeros_like(kv_ref)
        adj_ref[...] = jnp.zeros_like(adj_ref)

    factor = f_ref[...]
    for h in range(heads):
        qsc = (q_ref[:, h, :].astype(F32) * factor).astype(BF16)
        kv_ref[h] += dot_tn(k_ref[:, h, :], v_ref[:, h, :])
        adj_ref[h] += dot_tn(d_ref[:, h, :], qsc)


def main_kernel(first, heads, aliased, q_ref, k_ref, v_ref, d_ref, f_ref, before_ref, rest_ref, *refs):
    if aliased:
        refs = refs[1:]
    a_ref, qg_ref, kg_ref, vg_ref, state, suffix = refs
    @pl.when(pl.program_id(0) == 0)
    def _():
        state[...] = before_ref[...]
        suffix[...] = rest_ref[...]

    factor = f_ref[...]
    span = factor.shape[0]
    row = lax.broadcasted_iota(jnp.int32, (span, span), 0)
    col = lax.broadcasted_iota(jnp.int32, (span, span), 1)
    causal = row >= col
    for h in range(heads):
        q = q_ref[:, h, :]
        k = k_ref[:, h, :]
        v = v_ref[:, h, :]
        d = d_ref[:, h, :]
        qsc = (q.astype(F32) * factor).astype(BF16)
        prev = state[h]
        state_low = prev.astype(BF16)
        state[h] = prev + dot_tn(k, v)
        rest = suffix[h] - dot_tn(d, qsc)
        suffix[h] = rest
        suffix_low = rest.astype(BF16)
        scores = jnp.where(causal, dot_nt(qsc, k), 0.0).astype(BF16)
        adj_scores = jnp.where(causal, dot_nt(d, v), 0.0).astype(BF16)
        a_ref[:, h, :] = (dot_nn(qsc, state_low) + dot_nn(scores, v)).astype(a_ref.dtype)
        qg_ref[:, h, :] = ((dot_nt(d, state_low) + dot_nn(adj_scores, k)) * factor).astype(qg_ref.dtype)
        kg_ref[:, h, :] = (dot_nn(v, suffix_low) + dot_tn(adj_scores, qsc)).astype(kg_ref.dtype)
        vg_ref[:, h, :] = (dot_nt(k, suffix_low) + dot_tn(scores, d)).astype(vg_ref.dtype)


def exclusive_scan(total, axis, count, reverse):
    carried = jnp.zeros_like(total)
    acc = jnp.zeros_like(total)
    for hop in range(count - 1):
        pair = (count - 1 - hop, count - 2 - hop) if reverse else (hop, hop + 1)
        got = lax.ppermute(carried + total, axis, perm=[pair])
        acc = acc + got
        carried = got
    return acc


def per_device(queries, key_rows, value_rows, out_adjoint, seq_count):
    tok_dev, heads, head_dim = queries.shape
    span = SPAN
    blocks = tok_dev // span
    offset = lax.axis_index("seq") * tok_dev
    position = offset + jnp.arange(tok_dev, dtype=jnp.int32)
    factor = lax.rsqrt(jnp.float32(head_dim) * (position + 1).astype(jnp.float32))[:, None]

    tile = pl.BlockSpec((span, heads, head_dim), lambda c: (c, 0, 0))
    fac = pl.BlockSpec((span, 1), lambda c: (c, 0))
    whole = pl.BlockSpec((heads, head_dim, head_dim), lambda c: (0, 0, 0))
    state_shape = jax.ShapeDtypeStruct((heads, head_dim, head_dim), F32)
    kv_total, adj_total = pl.pallas_call(
        functools.partial(totals_kernel, heads),
        grid=(blocks,),
        in_specs=[tile, tile, tile, tile, fac],
        out_specs=[whole, whole],
        out_shape=[state_shape, state_shape],
        compiler_params=pltpu.CompilerParams(dimension_semantics=("arbitrary",)),
    )(queries, key_rows, value_rows, out_adjoint, factor)

    before = exclusive_scan(kv_total, "seq", seq_count, False)
    after = exclusive_scan(adj_total, "seq", seq_count, True)
    rest = after + adj_total

    width = 8 if heads % 8 == 0 and heads > 8 else heads
    groups = heads // width
    attended = None
    grads = []
    for g in range(groups):
        sel = slice(g * width, (g + 1) * width)
        before = exclusive_scan(kv_total[sel], "seq", seq_count, False)
        rest = exclusive_scan(adj_total[sel], "seq", seq_count, True) + adj_total[sel]
        gtile = pl.BlockSpec((span, width, head_dim), lambda c, g=g: (c, g, 0))
        gwhole = pl.BlockSpec((width, head_dim, head_dim), lambda c: (0, 0, 0))
        grad_shape = jax.ShapeDtypeStruct((tok_dev, width, head_dim), BF16)
        args = [queries, key_rows, value_rows, out_adjoint, factor, before, rest]
        specs = [gtile] * 4 + [fac, gwhole, gwhole]
        aliases = {}
        if attended is not None:
            args.append(attended)
            specs.append(pl.BlockSpec(memory_space=pl.ANY))
            aliases = {7: 0}
        outs = pl.pallas_call(
            functools.partial(main_kernel, g * width, width, attended is not None),
            grid=(blocks,),
            in_specs=specs,
            out_specs=[gtile] + [pl.BlockSpec((span, width, head_dim), lambda c: (c, 0, 0))] * 3,
            out_shape=[jax.ShapeDtypeStruct((tok_dev, heads, head_dim), BF16)] + [grad_shape] * 3,
            scratch_shapes=[pltpu.VMEM((width, head_dim, head_dim), F32)] * 2,
            input_output_aliases=aliases,
            compiler_params=pltpu.CompilerParams(dimension_semantics=("arbitrary",)),
        )(*args)
        attended = outs[0]
        grads.append([
            lax.all_to_all(x, ("head", "sub"), split_axis=0, concat_axis=1, tiled=True)
            for x in outs[1:]
        ])
    if groups == 1:
        outs = tuple(grads[0])
    else:
        outs = tuple(
            jnp.stack([grads[g][i].reshape(grads[g][i].shape[0], -1, width, head_dim)
                       for g in range(groups)], 2).reshape(grads[0][i].shape[0], -1, head_dim)
            for i in range(3)
        )
    return (attended,) + outs


def solution(mesh):
    seq_count = mesh.shape["seq"]
    spec_in = P(("grp", "seq"), ("head", "sub"), None)
    spec_grad = P(("grp", "seq", "head", "sub"), None, None)
    return jax.shard_map(
        lambda *a: per_device(*a, seq_count),
        mesh=mesh,
        in_specs=(spec_in,) * 4,
        out_specs=(spec_in, spec_grad, spec_grad, spec_grad),
        check_vma=False,
    )
```

```python
import functools

import jax
import jax.numpy as jnp
from jax import lax
from jax.experimental import pallas as pl
from jax.experimental.pallas import tpu as pltpu
from jax.sharding import PartitionSpec as P

SPAN = 64
F32 = jnp.float32
BF16 = jnp.bfloat16


def dot_nn(a, b):
    return jnp.dot(a, b, preferred_element_type=F32)


def dot_nt(a, b):
    return lax.dot_general(a, b, (((1,), (1,)), ((), ())), preferred_element_type=F32)


def dot_tn(a, b):
    return lax.dot_general(a, b, (((0,), (0,)), ((), ())), preferred_element_type=F32)


def totals_kernel(heads, q_ref, k_ref, v_ref, d_ref, f_ref, kv_ref, adj_ref):
    @pl.when(pl.program_id(0) == 0)
    def _():
        kv_ref[...] = jnp.zeros_like(kv_ref)
        adj_ref[...] = jnp.zeros_like(adj_ref)

    factor = f_ref[...]
    for h in range(heads):
        qsc = (q_ref[:, h, :].astype(F32) * factor).astype(BF16)
        kv_ref[h] += dot_tn(k_ref[:, h, :], v_ref[:, h, :])
        adj_ref[h] += dot_tn(d_ref[:, h, :], qsc)


def main_kernel(first, heads, aliased, q_ref, k_ref, v_ref, d_ref, f_ref, before_ref, rest_ref, *refs):
    if aliased:
        refs = refs[1:]
    a_ref, qg_ref, kg_ref, vg_ref, state, suffix = refs
    @pl.when(pl.program_id(0) == 0)
    def _():
        state[...] = before_ref[...]
        suffix[...] = rest_ref[...]

    factor = f_ref[...]
    span = factor.shape[0]
    row = lax.broadcasted_iota(jnp.int32, (span, span), 0)
    col = lax.broadcasted_iota(jnp.int32, (span, span), 1)
    causal = row >= col
    for h in range(heads):
        q = q_ref[:, h, :]
        k = k_ref[:, h, :]
        v = v_ref[:, h, :]
        d = d_ref[:, h, :]
        qsc = (q.astype(F32) * factor).astype(BF16)
        prev = state[h]
        state_low = prev.astype(BF16)
        state[h] = prev + dot_tn(k, v)
        rest = suffix[h] - dot_tn(d, qsc)
        suffix[h] = rest
        suffix_low = rest.astype(BF16)
        scores = jnp.where(causal, dot_nt(qsc, k), 0.0).astype(BF16)
        adj_scores = jnp.where(causal, dot_nt(d, v), 0.0).astype(BF16)
        a_ref[:, h, :] = (dot_nn(qsc, state_low) + dot_nn(scores, v)).astype(a_ref.dtype)
        qg_ref[:, h, :] = ((dot_nt(d, state_low) + dot_nn(adj_scores, k)) * factor).astype(qg_ref.dtype)
        kg_ref[:, h, :] = (dot_nn(v, suffix_low) + dot_tn(adj_scores, qsc)).astype(kg_ref.dtype)
        vg_ref[:, h, :] = (dot_nt(k, suffix_low) + dot_tn(scores, d)).astype(vg_ref.dtype)


def interleave_kernel(groups, *refs):
    o_ref = refs[groups]
    g = pl.program_id(1)
    for i in range(groups):
        @pl.when(g == i)
        def _():
            o_ref[...] = refs[i][...]


def interleave(parts):
    peers, tok, width, head_dim = parts[0].shape
    groups = len(parts)
    nbytes = 2 * groups * peers * tok * width * head_dim * parts[0].dtype.itemsize
    return pl.pallas_call(
        functools.partial(interleave_kernel, groups),
        grid=(peers, groups),
        in_specs=[pl.BlockSpec((None, tok, width, head_dim), lambda j, g: (j, 0, 0, 0))] * groups,
        out_specs=pl.BlockSpec((tok, width, head_dim), lambda j, g: (0, j * groups + g, 0)),
        out_shape=jax.ShapeDtypeStruct((tok, peers * groups * width, head_dim), parts[0].dtype),
        cost_estimate=pl.CostEstimate(flops=0, transcendentals=0, bytes_accessed=nbytes),
    )(*parts)


def exclusive_scan(total, axis, count, reverse):
    carried = jnp.zeros_like(total)
    acc = jnp.zeros_like(total)
    for hop in range(count - 1):
        pair = (count - 1 - hop, count - 2 - hop) if reverse else (hop, hop + 1)
        got = lax.ppermute(carried + total, axis, perm=[pair])
        acc = acc + got
        carried = got
    return acc


def per_device(queries, key_rows, value_rows, out_adjoint, seq_count):
    tok_dev, heads, head_dim = queries.shape
    span = SPAN
    blocks = tok_dev // span
    offset = lax.axis_index("seq") * tok_dev
    position = offset + jnp.arange(tok_dev, dtype=jnp.int32)
    factor = lax.rsqrt(jnp.float32(head_dim) * (position + 1).astype(jnp.float32))[:, None]

    fac = pl.BlockSpec((span, 1), lambda c: (c, 0))
    width = 8 if heads % 8 == 0 and heads > 8 else heads
    groups = heads // width
    peers = lax.psum(1, ("head", "sub"))
    attended = None
    grads = []
    for g in range(groups):
        gtile = pl.BlockSpec((span, width, head_dim), lambda c, g=g: (c, g, 0))
        gwhole = pl.BlockSpec((width, head_dim, head_dim), lambda c: (0, 0, 0))
        state_shape = jax.ShapeDtypeStruct((width, head_dim, head_dim), F32)
        kv_total, adj_total = pl.pallas_call(
            functools.partial(totals_kernel, width),
            grid=(blocks,),
            in_specs=[gtile] * 4 + [fac],
            out_specs=[gwhole, gwhole],
            out_shape=[state_shape, state_shape],
            compiler_params=pltpu.CompilerParams(dimension_semantics=("arbitrary",)),
        )(queries, key_rows, value_rows, out_adjoint, factor)
        before = exclusive_scan(kv_total, "seq", seq_count, False)
        rest = exclusive_scan(adj_total, "seq", seq_count, True) + adj_total
        grad_shape = jax.ShapeDtypeStruct((tok_dev, width, head_dim), BF16)
        args = [queries, key_rows, value_rows, out_adjoint, factor, before, rest]
        specs = [gtile] * 4 + [fac, gwhole, gwhole]
        aliases = {}
        if attended is not None:
            args.append(attended)
            specs.append(pl.BlockSpec(memory_space=pl.ANY))
            aliases = {7: 0}
        outs = pl.pallas_call(
            functools.partial(main_kernel, g * width, width, attended is not None),
            grid=(blocks,),
            in_specs=specs,
            out_specs=[gtile] + [pl.BlockSpec((span, width, head_dim), lambda c: (c, 0, 0))] * 3,
            out_shape=[jax.ShapeDtypeStruct((tok_dev, heads, head_dim), BF16)] + [grad_shape] * 3,
            scratch_shapes=[pltpu.VMEM((width, head_dim, head_dim), F32)] * 2,
            input_output_aliases=aliases,
            compiler_params=pltpu.CompilerParams(dimension_semantics=("arbitrary",)),
        )(*args)
        attended = outs[0]
        if width % 8:
            grads.append([
                lax.all_to_all(x, ("head", "sub"), split_axis=0, concat_axis=1, tiled=True)
                for x in outs[1:]
            ])
        else:
            grads.append([
                lax.all_to_all(
                    x.reshape(peers, tok_dev // peers, width, head_dim), ("head", "sub"),
                    split_axis=0, concat_axis=0, tiled=True,
                )
                for x in outs[1:]
            ])
    if width % 8:
        outs = tuple(grads[0])
    else:
        outs = tuple(interleave([grads[g][i] for g in range(groups)]) for i in range(3))
    return (attended,) + outs


def solution(mesh):
    seq_count = mesh.shape["seq"]
    spec_in = P(("grp", "seq"), ("head", "sub"), None)
    spec_grad = P(("grp", "seq", "head", "sub"), None, None)
    return jax.shard_map(
        lambda *a: per_device(*a, seq_count),
        mesh=mesh,
        in_specs=(spec_in,) * 4,
        out_specs=(spec_in, spec_grad, spec_grad, spec_grad),
        check_vma=False,
    )
```

```python
import functools

import jax
import jax.numpy as jnp
from jax import lax
from jax.experimental import pallas as pl
from jax.experimental.pallas import tpu as pltpu
from jax.sharding import PartitionSpec as P

SPAN = 64
F32 = jnp.float32
BF16 = jnp.bfloat16


def dot_nn(a, b):
    return jnp.dot(a, b, preferred_element_type=F32)


def dot_nt(a, b):
    return lax.dot_general(a, b, (((1,), (1,)), ((), ())), preferred_element_type=F32)


def dot_tn(a, b):
    return lax.dot_general(a, b, (((0,), (0,)), ((), ())), preferred_element_type=F32)


def totals_kernel(heads, q_ref, k_ref, v_ref, d_ref, f_ref, kv_ref, adj_ref):
    @pl.when(pl.program_id(0) == 0)
    def _():
        kv_ref[...] = jnp.zeros_like(kv_ref)
        adj_ref[...] = jnp.zeros_like(adj_ref)

    factor = f_ref[...]
    for h in range(heads):
        qsc = (q_ref[:, h, :].astype(F32) * factor).astype(BF16)
        kv_ref[h] += dot_tn(k_ref[:, h, :], v_ref[:, h, :])
        adj_ref[h] += dot_tn(d_ref[:, h, :], qsc)


def main_kernel(first, heads, aliased, q_ref, k_ref, v_ref, d_ref, f_ref, before_ref, rest_ref, *refs):
    if aliased:
        refs = refs[1:]
    a_ref, qg_ref, kg_ref, vg_ref, state, suffix = refs
    @pl.when(pl.program_id(0) == 0)
    def _():
        state[...] = before_ref[...]
        suffix[...] = rest_ref[...]

    factor = f_ref[...]
    span = factor.shape[0]
    row = lax.broadcasted_iota(jnp.int32, (span, span), 0)
    col = lax.broadcasted_iota(jnp.int32, (span, span), 1)
    causal = row >= col
    for h in range(heads):
        q = q_ref[:, h, :]
        k = k_ref[:, h, :]
        v = v_ref[:, h, :]
        d = d_ref[:, h, :]
        qsc = (q.astype(F32) * factor).astype(BF16)
        prev = state[h]
        state_low = prev.astype(BF16)
        state[h] = prev + dot_tn(k, v)
        rest = suffix[h] - dot_tn(d, qsc)
        suffix[h] = rest
        suffix_low = rest.astype(BF16)
        scores = jnp.where(causal, dot_nt(qsc, k), 0.0).astype(BF16)
        adj_scores = jnp.where(causal, dot_nt(d, v), 0.0).astype(BF16)
        a_ref[:, h, :] = (dot_nn(qsc, state_low) + dot_nn(scores, v)).astype(a_ref.dtype)
        qg_ref[:, h, :] = ((dot_nt(d, state_low) + dot_nn(adj_scores, k)) * factor).astype(qg_ref.dtype)
        kg_ref[:, h, :] = (dot_nn(v, suffix_low) + dot_tn(adj_scores, qsc)).astype(kg_ref.dtype)
        vg_ref[:, h, :] = (dot_nt(k, suffix_low) + dot_tn(scores, d)).astype(vg_ref.dtype)


def skewed_scan(first, second, axis, count, reverse):
    place = lax.axis_index(axis)
    pos = count - 1 - place if reverse else place
    dev = (lambda i: count - 1 - i) if reverse else (lambda i: i)
    got_first = jnp.zeros_like(first)
    got_second = jnp.zeros_like(second)
    for step in range(count):
        pairs = []
        if step + 1 < count:
            pairs.append((dev(step), dev(step + 1)))
        if step >= 1:
            pairs.append((dev(step - 1), dev(step)))
        send = jnp.where(pos == step, got_first + first, got_second + second)
        got = lax.ppermute(send, axis, perm=pairs)
        if step + 1 < count:
            got_first = got_first + jnp.where(pos == step + 1, got, 0.0)
        if step >= 1:
            got_second = got_second + jnp.where(pos == step, got, 0.0)
    return got_first, got_second


def exclusive_scan(total, axis, count, reverse):
    carried = jnp.zeros_like(total)
    acc = jnp.zeros_like(total)
    for hop in range(count - 1):
        pair = (count - 1 - hop, count - 2 - hop) if reverse else (hop, hop + 1)
        got = lax.ppermute(carried + total, axis, perm=[pair])
        acc = acc + got
        carried = got
    return acc


def per_device(queries, key_rows, value_rows, out_adjoint, seq_count):
    tok_dev, heads, head_dim = queries.shape
    span = SPAN
    blocks = tok_dev // span
    offset = lax.axis_index("seq") * tok_dev
    position = offset + jnp.arange(tok_dev, dtype=jnp.int32)
    factor = lax.rsqrt(jnp.float32(head_dim) * (position + 1).astype(jnp.float32))[:, None]

    tile = pl.BlockSpec((span, heads, head_dim), lambda c: (c, 0, 0))
    fac = pl.BlockSpec((span, 1), lambda c: (c, 0))
    whole = pl.BlockSpec((heads, head_dim, head_dim), lambda c: (0, 0, 0))
    state_shape = jax.ShapeDtypeStruct((heads, head_dim, head_dim), F32)
    kv_total, adj_total = pl.pallas_call(
        functools.partial(totals_kernel, heads),
        grid=(blocks,),
        in_specs=[tile, tile, tile, tile, fac],
        out_specs=[whole, whole],
        out_shape=[state_shape, state_shape],
        compiler_params=pltpu.CompilerParams(dimension_semantics=("arbitrary",)),
    )(queries, key_rows, value_rows, out_adjoint, factor)

    before = exclusive_scan(kv_total, "seq", seq_count, False)
    after = exclusive_scan(adj_total, "seq", seq_count, True)
    rest = after + adj_total

    width = 8 if heads % 8 == 0 and heads > 8 else heads
    groups = heads // width
    attended = None
    grads = []
    if groups == 2:
        befores = skewed_scan(kv_total[:width], kv_total[width:], "seq", seq_count, False)
        afters = skewed_scan(adj_total[:width], adj_total[width:], "seq", seq_count, True)
    for g in range(groups):
        sel = slice(g * width, (g + 1) * width)
        if groups == 2:
            before = befores[g]
            rest = afters[g] + adj_total[sel]
        else:
            before = exclusive_scan(kv_total[sel], "seq", seq_count, False)
            rest = exclusive_scan(adj_total[sel], "seq", seq_count, True) + adj_total[sel]
        gtile = pl.BlockSpec((span, width, head_dim), lambda c, g=g: (c, g, 0))
        gwhole = pl.BlockSpec((width, head_dim, head_dim), lambda c: (0, 0, 0))
        grad_shape = jax.ShapeDtypeStruct((tok_dev, width, head_dim), BF16)
        args = [queries, key_rows, value_rows, out_adjoint, factor, before, rest]
        specs = [gtile] * 4 + [fac, gwhole, gwhole]
        aliases = {}
        if attended is not None:
            args.append(attended)
            specs.append(pl.BlockSpec(memory_space=pl.ANY))
            aliases = {7: 0}
        outs = pl.pallas_call(
            functools.partial(main_kernel, g * width, width, attended is not None),
            grid=(blocks,),
            in_specs=specs,
            out_specs=[gtile] + [pl.BlockSpec((span, width, head_dim), lambda c: (c, 0, 0))] * 3,
            out_shape=[jax.ShapeDtypeStruct((tok_dev, heads, head_dim), BF16)] + [grad_shape] * 3,
            scratch_shapes=[pltpu.VMEM((width, head_dim, head_dim), F32)] * 2,
            input_output_aliases=aliases,
            compiler_params=pltpu.CompilerParams(dimension_semantics=("arbitrary",)),
        )(*args)
        attended = outs[0]
        grads.append([
            lax.all_to_all(x, ("head", "sub"), split_axis=0, concat_axis=1, tiled=True)
            for x in outs[1:]
        ])
    if groups == 1:
        outs = tuple(grads[0])
    else:
        outs = tuple(
            jnp.stack([grads[g][i].reshape(grads[g][i].shape[0], -1, width, head_dim)
                       for g in range(groups)], 2).reshape(grads[0][i].shape[0], -1, head_dim)
            for i in range(3)
        )
    return (attended,) + outs


def solution(mesh):
    seq_count = mesh.shape["seq"]
    spec_in = P(("grp", "seq"), ("head", "sub"), None)
    spec_grad = P(("grp", "seq", "head", "sub"), None, None)
    return jax.shard_map(
        lambda *a: per_device(*a, seq_count),
        mesh=mesh,
        in_specs=(spec_in,) * 4,
        out_specs=(spec_in, spec_grad, spec_grad, spec_grad),
        check_vma=False,
    )
```

```python
import functools

import jax
import jax.numpy as jnp
from jax import lax
from jax.experimental import pallas as pl
from jax.experimental.pallas import tpu as pltpu
from jax.sharding import PartitionSpec as P

SPAN = 64
F32 = jnp.float32
BF16 = jnp.bfloat16


def dot_nn(a, b):
    return jnp.dot(a, b, preferred_element_type=F32)


def dot_nt(a, b):
    return lax.dot_general(a, b, (((1,), (1,)), ((), ())), preferred_element_type=F32)


def dot_tn(a, b):
    return lax.dot_general(a, b, (((0,), (0,)), ((), ())), preferred_element_type=F32)


def totals_kernel(heads, q_ref, k_ref, v_ref, d_ref, f_ref, kv_ref, adj_ref):
    @pl.when(pl.program_id(0) == 0)
    def _():
        kv_ref[...] = jnp.zeros_like(kv_ref)
        adj_ref[...] = jnp.zeros_like(adj_ref)

    factor = f_ref[...]
    for h in range(heads):
        qsc = (q_ref[:, h, :].astype(F32) * factor).astype(BF16)
        kv_ref[h] += dot_tn(k_ref[:, h, :], v_ref[:, h, :])
        adj_ref[h] += dot_tn(d_ref[:, h, :], qsc)


def main_kernel(first, heads, aliased, q_ref, k_ref, v_ref, d_ref, f_ref, before_ref, rest_ref, *refs):
    if aliased:
        refs = refs[1:]
    a_ref, qg_ref, kg_ref, vg_ref, state, suffix = refs
    @pl.when(pl.program_id(0) == 0)
    def _():
        state[...] = before_ref[...]
        suffix[...] = rest_ref[...]

    factor = f_ref[...]
    span = factor.shape[0]
    row = lax.broadcasted_iota(jnp.int32, (span, span), 0)
    col = lax.broadcasted_iota(jnp.int32, (span, span), 1)
    causal = row >= col
    upper = row <= col
    for h in range(heads):
        q = q_ref[:, h, :]
        k = k_ref[:, h, :]
        v = v_ref[:, h, :]
        d = d_ref[:, h, :]
        qsc = (q.astype(F32) * factor).astype(BF16)
        prev = state[h]
        state_low = prev.astype(BF16)
        state[h] = prev + dot_tn(k, v)
        rest = suffix[h] - dot_tn(d, qsc)
        suffix[h] = rest
        suffix_low = rest.astype(BF16)
        scores = jnp.where(causal, dot_nt(qsc, k), 0.0).astype(BF16)
        adj_scores = jnp.where(causal, dot_nt(d, v), 0.0).astype(BF16)
        a_ref[:, h, :] = (dot_nn(qsc, state_low) + dot_nn(scores, v)).astype(a_ref.dtype)
        qg_ref[:, h, :] = ((dot_nt(d, state_low) + dot_nn(adj_scores, k)) * factor).astype(qg_ref.dtype)
        adj_scores_t = jnp.where(upper, dot_nt(v, d), 0.0).astype(BF16)
        scores_t = jnp.where(upper, dot_nt(k, qsc), 0.0).astype(BF16)
        kg_ref[:, h, :] = (dot_nn(v, suffix_low) + dot_nn(adj_scores_t, qsc)).astype(kg_ref.dtype)
        vg_ref[:, h, :] = (dot_nt(k, suffix_low) + dot_nn(scores_t, d)).astype(vg_ref.dtype)


def exclusive_scan(total, axis, count, reverse):
    carried = jnp.zeros_like(total)
    acc = jnp.zeros_like(total)
    for hop in range(count - 1):
        pair = (count - 1 - hop, count - 2 - hop) if reverse else (hop, hop + 1)
        got = lax.ppermute(carried + total, axis, perm=[pair])
        acc = acc + got
        carried = got
    return acc


def per_device(queries, key_rows, value_rows, out_adjoint, seq_count):
    tok_dev, heads, head_dim = queries.shape
    span = SPAN
    blocks = tok_dev // span
    offset = lax.axis_index("seq") * tok_dev
    position = offset + jnp.arange(tok_dev, dtype=jnp.int32)
    factor = lax.rsqrt(jnp.float32(head_dim) * (position + 1).astype(jnp.float32))[:, None]

    tile = pl.BlockSpec((span, heads, head_dim), lambda c: (c, 0, 0))
    fac = pl.BlockSpec((span, 1), lambda c: (c, 0))
    whole = pl.BlockSpec((heads, head_dim, head_dim), lambda c: (0, 0, 0))
    state_shape = jax.ShapeDtypeStruct((heads, head_dim, head_dim), F32)
    kv_total, adj_total = pl.pallas_call(
        functools.partial(totals_kernel, heads),
        grid=(blocks,),
        in_specs=[tile, tile, tile, tile, fac],
        out_specs=[whole, whole],
        out_shape=[state_shape, state_shape],
        compiler_params=pltpu.CompilerParams(dimension_semantics=("arbitrary",)),
    )(queries, key_rows, value_rows, out_adjoint, factor)

    before = exclusive_scan(kv_total, "seq", seq_count, False)
    after = exclusive_scan(adj_total, "seq", seq_count, True)
    rest = after + adj_total

    width = 8 if heads % 8 == 0 and heads > 8 else heads
    groups = heads // width
    attended = None
    grads = []
    for g in range(groups):
        sel = slice(g * width, (g + 1) * width)
        before = exclusive_scan(kv_total[sel], "seq", seq_count, False)
        rest = exclusive_scan(adj_total[sel], "seq", seq_count, True) + adj_total[sel]
        gtile = pl.BlockSpec((span, width, head_dim), lambda c, g=g: (c, g, 0))
        gwhole = pl.BlockSpec((width, head_dim, head_dim), lambda c: (0, 0, 0))
        grad_shape = jax.ShapeDtypeStruct((tok_dev, width, head_dim), BF16)
        args = [queries, key_rows, value_rows, out_adjoint, factor, before, rest]
        specs = [gtile] * 4 + [fac, gwhole, gwhole]
        aliases = {}
        if attended is not None:
            args.append(attended)
            specs.append(pl.BlockSpec(memory_space=pl.ANY))
            aliases = {7: 0}
        outs = pl.pallas_call(
            functools.partial(main_kernel, g * width, width, attended is not None),
            grid=(blocks,),
            in_specs=specs,
            out_specs=[gtile] + [pl.BlockSpec((span, width, head_dim), lambda c: (c, 0, 0))] * 3,
            out_shape=[jax.ShapeDtypeStruct((tok_dev, heads, head_dim), BF16)] + [grad_shape] * 3,
            scratch_shapes=[pltpu.VMEM((width, head_dim, head_dim), F32)] * 2,
            input_output_aliases=aliases,
            compiler_params=pltpu.CompilerParams(dimension_semantics=("arbitrary",)),
        )(*args)
        attended = outs[0]
        grads.append([
            lax.all_to_all(x, ("head", "sub"), split_axis=0, concat_axis=1, tiled=True)
            for x in outs[1:]
        ])
    if groups == 1:
        outs = tuple(grads[0])
    else:
        outs = tuple(
            jnp.stack([grads[g][i].reshape(grads[g][i].shape[0], -1, width, head_dim)
                       for g in range(groups)], 2).reshape(grads[0][i].shape[0], -1, head_dim)
            for i in range(3)
        )
    return (attended,) + outs


def solution(mesh):
    seq_count = mesh.shape["seq"]
    spec_in = P(("grp", "seq"), ("head", "sub"), None)
    spec_grad = P(("grp", "seq", "head", "sub"), None, None)
    return jax.shard_map(
        lambda *a: per_device(*a, seq_count),
        mesh=mesh,
        in_specs=(spec_in,) * 4,
        out_specs=(spec_in, spec_grad, spec_grad, spec_grad),
        check_vma=False,
    )
```

```python
import functools

import jax
import jax.numpy as jnp
from jax import lax
from jax.experimental import pallas as pl
from jax.experimental.pallas import tpu as pltpu
from jax.sharding import PartitionSpec as P

SPAN = 64
F32 = jnp.float32
BF16 = jnp.bfloat16


def dot_nn(a, b):
    return jnp.dot(a, b, preferred_element_type=F32)


def dot_nt(a, b):
    return lax.dot_general(a, b, (((1,), (1,)), ((), ())), preferred_element_type=F32)


def dot_tn(a, b):
    return lax.dot_general(a, b, (((0,), (0,)), ((), ())), preferred_element_type=F32)


def totals_kernel(heads, q_ref, k_ref, v_ref, d_ref, f_ref, kv_ref, adj_ref):
    factor = f_ref[...]
    for h in range(heads):
        qsc = (q_ref[:, h, :].astype(F32) * factor).astype(BF16)
        kv_ref[h] = dot_tn(k_ref[:, h, :], v_ref[:, h, :])
        adj_ref[h] = dot_tn(d_ref[:, h, :], qsc)


def main_kernel(first, heads, aliased, q_ref, k_ref, v_ref, d_ref, f_ref, before_ref, rest_ref, *refs):
    if aliased:
        refs = refs[1:]
    a_ref, qg_ref, kg_ref, vg_ref, state, suffix = refs
    @pl.when(pl.program_id(0) == 0)
    def _():
        state[...] = before_ref[...]
        suffix[...] = rest_ref[...]

    factor = f_ref[...]
    span = factor.shape[0]
    row = lax.broadcasted_iota(jnp.int32, (span, span), 0)
    col = lax.broadcasted_iota(jnp.int32, (span, span), 1)
    causal = row >= col
    for h in range(heads):
        q = q_ref[:, h, :]
        k = k_ref[:, h, :]
        v = v_ref[:, h, :]
        d = d_ref[:, h, :]
        qsc = (q.astype(F32) * factor).astype(BF16)
        prev = state[h]
        state_low = prev.astype(BF16)
        state[h] = prev + dot_tn(k, v)
        rest = suffix[h] - dot_tn(d, qsc)
        suffix[h] = rest
        suffix_low = rest.astype(BF16)
        scores = jnp.where(causal, dot_nt(qsc, k), 0.0).astype(BF16)
        adj_scores = jnp.where(causal, dot_nt(d, v), 0.0).astype(BF16)
        a_ref[:, h, :] = (dot_nn(qsc, state_low) + dot_nn(scores, v)).astype(a_ref.dtype)
        qg_ref[:, h, :] = ((dot_nt(d, state_low) + dot_nn(adj_scores, k)) * factor).astype(qg_ref.dtype)
        kg_ref[:, h, :] = (dot_nn(v, suffix_low) + dot_tn(adj_scores, qsc)).astype(kg_ref.dtype)
        vg_ref[:, h, :] = (dot_nt(k, suffix_low) + dot_tn(scores, d)).astype(vg_ref.dtype)


def exclusive_scan(total, axis, count, reverse):
    carried = jnp.zeros_like(total)
    acc = jnp.zeros_like(total)
    for hop in range(count - 1):
        pair = (count - 1 - hop, count - 2 - hop) if reverse else (hop, hop + 1)
        got = lax.ppermute(carried + total, axis, perm=[pair])
        acc = acc + got
        carried = got
    return acc


def per_device(queries, key_rows, value_rows, out_adjoint, seq_count):
    tok_dev, heads, head_dim = queries.shape
    span = SPAN
    blocks = tok_dev // span
    offset = lax.axis_index("seq") * tok_dev
    position = offset + jnp.arange(tok_dev, dtype=jnp.int32)
    factor = lax.rsqrt(jnp.float32(head_dim) * (position + 1).astype(jnp.float32))[:, None]

    fac = pl.BlockSpec((span, 1), lambda c: (c, 0))
    width = 8 if heads % 8 == 0 and heads > 8 else heads
    state_shape = jax.ShapeDtypeStruct((heads, head_dim, head_dim), F32)
    rows = pl.BlockSpec((tok_dev, width, head_dim), lambda g: (0, g, 0))
    group_state = pl.BlockSpec((width, head_dim, head_dim), lambda g: (g, 0, 0))
    kv_total, adj_total = pl.pallas_call(
        functools.partial(totals_kernel, width),
        grid=(heads // width,),
        in_specs=[rows] * 4 + [pl.BlockSpec((tok_dev, 1), lambda g: (0, 0))],
        out_specs=[group_state, group_state],
        out_shape=[state_shape, state_shape],
    )(queries, key_rows, value_rows, out_adjoint, factor)

    groups = heads // width
    attended = None
    grads = []
    for g in range(groups):
        sel = slice(g * width, (g + 1) * width)
        before = exclusive_scan(kv_total[sel], "seq", seq_count, False)
        rest = exclusive_scan(adj_total[sel], "seq", seq_count, True) + adj_total[sel]
        gtile = pl.BlockSpec((span, width, head_dim), lambda c, g=g: (c, g, 0))
        gwhole = pl.BlockSpec((width, head_dim, head_dim), lambda c: (0, 0, 0))
        grad_shape = jax.ShapeDtypeStruct((tok_dev, width, head_dim), BF16)
        args = [queries, key_rows, value_rows, out_adjoint, factor, before, rest]
        specs = [gtile] * 4 + [fac, gwhole, gwhole]
        aliases = {}
        if attended is not None:
            args.append(attended)
            specs.append(pl.BlockSpec(memory_space=pl.ANY))
            aliases = {7: 0}
        outs = pl.pallas_call(
            functools.partial(main_kernel, g * width, width, attended is not None),
            grid=(blocks,),
            in_specs=specs,
            out_specs=[gtile] + [pl.BlockSpec((span, width, head_dim), lambda c: (c, 0, 0))] * 3,
            out_shape=[jax.ShapeDtypeStruct((tok_dev, heads, head_dim), BF16)] + [grad_shape] * 3,
            scratch_shapes=[pltpu.VMEM((width, head_dim, head_dim), F32)] * 2,
            input_output_aliases=aliases,
            compiler_params=pltpu.CompilerParams(dimension_semantics=("arbitrary",)),
        )(*args)
        attended = outs[0]
        grads.append([
            lax.all_to_all(x, ("head", "sub"), split_axis=0, concat_axis=1, tiled=True)
            for x in outs[1:]
        ])
    if groups == 1:
        outs = tuple(grads[0])
    else:
        outs = tuple(
            jnp.stack([grads[g][i].reshape(grads[g][i].shape[0], -1, width, head_dim)
                       for g in range(groups)], 2).reshape(grads[0][i].shape[0], -1, head_dim)
            for i in range(3)
        )
    return (attended,) + outs


def solution(mesh):
    seq_count = mesh.shape["seq"]
    spec_in = P(("grp", "seq"), ("head", "sub"), None)
    spec_grad = P(("grp", "seq", "head", "sub"), None, None)
    return jax.shard_map(
        lambda *a: per_device(*a, seq_count),
        mesh=mesh,
        in_specs=(spec_in,) * 4,
        out_specs=(spec_in, spec_grad, spec_grad, spec_grad),
        check_vma=False,
    )
```

```python
import functools

import jax
import jax.numpy as jnp
from jax import lax
from jax.experimental import pallas as pl
from jax.experimental.pallas import tpu as pltpu
from jax.sharding import PartitionSpec as P

SPAN = 64
F32 = jnp.float32
BF16 = jnp.bfloat16


def dot_nn(a, b):
    return jnp.dot(a, b, preferred_element_type=F32)


def dot_nt(a, b):
    return lax.dot_general(a, b, (((1,), (1,)), ((), ())), preferred_element_type=F32)


def dot_tn(a, b):
    return lax.dot_general(a, b, (((0,), (0,)), ((), ())), preferred_element_type=F32)


def totals_kernel(heads, q_ref, k_ref, v_ref, d_ref, kv_ref, adj_ref):
    for h in range(heads):
        kv_ref[h] = dot_tn(k_ref[h], v_ref[h])
        adj_ref[h] = dot_tn(d_ref[h], q_ref[h])


def main_kernel(heads, aliased, q_ref, k_ref, v_ref, d_ref, f_ref, before_ref, rest_ref, *refs):
    if aliased:
        refs = refs[1:]
    a_ref, qg_ref, kg_ref, vg_ref, state, suffix = refs

    @pl.when(pl.program_id(0) == 0)
    def _():
        state[...] = before_ref[...]
        suffix[...] = rest_ref[...]

    factor = f_ref[...]
    span = factor.shape[0]
    row = lax.broadcasted_iota(jnp.int32, (span, span), 0)
    col = lax.broadcasted_iota(jnp.int32, (span, span), 1)
    causal = row >= col
    for h in range(heads):
        qsc = q_ref[h]
        k = k_ref[h]
        v = v_ref[h]
        d = d_ref[h]
        prev = state[h]
        state_low = prev.astype(BF16)
        state[h] = prev + dot_tn(k, v)
        rest = suffix[h] - dot_tn(d, qsc)
        suffix[h] = rest
        suffix_low = rest.astype(BF16)
        scores = jnp.where(causal, dot_nt(qsc, k), 0.0).astype(BF16)
        adj_scores = jnp.where(causal, dot_nt(d, v), 0.0).astype(BF16)
        a_ref[h] = (dot_nn(qsc, state_low) + dot_nn(scores, v)).astype(a_ref.dtype)
        qg_ref[h] = ((dot_nt(d, state_low) + dot_nn(adj_scores, k)) * factor).astype(qg_ref.dtype)
        kg_ref[h] = (dot_nn(v, suffix_low) + dot_tn(adj_scores, qsc)).astype(kg_ref.dtype)
        vg_ref[h] = (dot_nt(k, suffix_low) + dot_tn(scores, d)).astype(vg_ref.dtype)


def exclusive_scan(total, axis, count, reverse):
    carried = jnp.zeros_like(total)
    acc = jnp.zeros_like(total)
    for hop in range(count - 1):
        pair = (count - 1 - hop, count - 2 - hop) if reverse else (hop, hop + 1)
        got = lax.ppermute(carried + total, axis, perm=[pair])
        acc = acc + got
        carried = got
    return acc


def per_device(queries, key_rows, value_rows, out_adjoint, seq_count):
    tok_dev, heads, head_dim = queries.shape
    span = SPAN
    blocks = tok_dev // span
    offset = lax.axis_index("seq") * tok_dev
    position = offset + jnp.arange(tok_dev, dtype=jnp.int32)
    factor = lax.rsqrt(jnp.float32(head_dim) * (position + 1).astype(jnp.float32))[:, None]
    scaled = (queries.astype(F32) * factor[:, :, None]).astype(BF16)
    qh, kh, vh, dh = (jnp.transpose(x, (1, 0, 2)) for x in (scaled, key_rows, value_rows, out_adjoint))

    width = 8 if heads % 8 == 0 and heads > 8 else heads
    groups = heads // width
    state_shape = jax.ShapeDtypeStruct((heads, head_dim, head_dim), F32)
    rows = pl.BlockSpec((width, tok_dev, head_dim), lambda g: (g, 0, 0))
    group_state = pl.BlockSpec((width, head_dim, head_dim), lambda g: (g, 0, 0))
    kv_total, adj_total = pl.pallas_call(
        functools.partial(totals_kernel, width),
        grid=(groups,),
        in_specs=[rows] * 4,
        out_specs=[group_state, group_state],
        out_shape=[state_shape, state_shape],
    )(qh, kh, vh, dh)

    fac = pl.BlockSpec((span, 1), lambda c: (c, 0))
    peers = lax.psum(1, ("head", "sub"))
    attended = None
    grads = []
    for g in range(groups):
        sel = slice(g * width, (g + 1) * width)
        before = exclusive_scan(kv_total[sel], "seq", seq_count, False)
        rest = exclusive_scan(adj_total[sel], "seq", seq_count, True) + adj_total[sel]
        gtile = pl.BlockSpec((width, span, head_dim), lambda c, g=g: (g, c, 0))
        otile = pl.BlockSpec((width, span, head_dim), lambda c: (0, c, 0))
        gwhole = pl.BlockSpec((width, head_dim, head_dim), lambda c: (0, 0, 0))
        grad_shape = jax.ShapeDtypeStruct((width, tok_dev, head_dim), BF16)
        args = [qh, kh, vh, dh, factor, before, rest]
        specs = [gtile] * 4 + [fac, gwhole, gwhole]
        aliases = {}
        if attended is not None:
            args.append(attended)
            specs.append(pl.BlockSpec(memory_space=pl.ANY))
            aliases = {7: 0}
        outs = pl.pallas_call(
            functools.partial(main_kernel, width, attended is not None),
            grid=(blocks,),
            in_specs=specs,
            out_specs=[gtile] + [otile] * 3,
            out_shape=[jax.ShapeDtypeStruct((heads, tok_dev, head_dim), BF16)] + [grad_shape] * 3,
            scratch_shapes=[pltpu.VMEM((width, head_dim, head_dim), F32)] * 2,
            input_output_aliases=aliases,
            compiler_params=pltpu.CompilerParams(dimension_semantics=("arbitrary",)),
        )(*args)
        attended = outs[0]
        grads.append([
            lax.all_to_all(x, ("head", "sub"), split_axis=1, concat_axis=0, tiled=True)
            for x in outs[1:]
        ])
    tok_out = tok_dev // peers
    outs = tuple(
        jnp.transpose(
            jnp.stack([grads[g][i].reshape(peers, width, tok_out, head_dim) for g in range(groups)], 1)
            .reshape(heads * peers, tok_out, head_dim),
            (1, 0, 2),
        )
        for i in range(3)
    )
    return (jnp.transpose(attended, (1, 0, 2)),) + outs


def solution(mesh):
    seq_count = mesh.shape["seq"]
    spec_in = P(("grp", "seq"), ("head", "sub"), None)
    spec_grad = P(("grp", "seq", "head", "sub"), None, None)
    return jax.shard_map(
        lambda *a: per_device(*a, seq_count),
        mesh=mesh,
        in_specs=(spec_in,) * 4,
        out_specs=(spec_in, spec_grad, spec_grad, spec_grad),
        check_vma=False,
    )
```

```python
import functools

import jax
import jax.numpy as jnp
from jax import lax
from jax.experimental import pallas as pl
from jax.experimental.pallas import tpu as pltpu
from jax.sharding import PartitionSpec as P

SPAN = 64
F32 = jnp.float32
BF16 = jnp.bfloat16


def dot_nn(a, b):
    return jnp.dot(a, b, preferred_element_type=F32)


def dot_nt(a, b):
    return lax.dot_general(a, b, (((1,), (1,)), ((), ())), preferred_element_type=F32)


def dot_tn(a, b):
    return lax.dot_general(a, b, (((0,), (0,)), ((), ())), preferred_element_type=F32)


def totals_kernel(heads, q_ref, k_ref, v_ref, d_ref, kv_ref, adj_ref):
    for h in range(heads):
        kv_ref[h] = dot_tn(k_ref[h], v_ref[h])
        adj_ref[h] = dot_tn(d_ref[h], q_ref[h])


def main_kernel(heads, aliased, q_ref, k_ref, v_ref, d_ref, f_ref, before_ref, rest_ref, *refs):
    if aliased:
        refs = refs[1:]
    a_ref, qg_ref, kg_ref, vg_ref, state, suffix = refs

    @pl.when(pl.program_id(0) == 0)
    def _():
        state[...] = before_ref[...]
        suffix[...] = rest_ref[...]

    factor = f_ref[...]
    span = factor.shape[0]
    row = lax.broadcasted_iota(jnp.int32, (span, span), 0)
    col = lax.broadcasted_iota(jnp.int32, (span, span), 1)
    causal = row >= col
    for h in range(heads):
        qsc = q_ref[h]
        k = k_ref[h]
        v = v_ref[h]
        d = d_ref[h]
        prev = state[h]
        state_low = prev.astype(BF16)
        state[h] = prev + dot_tn(k, v)
        rest = suffix[h] - dot_tn(d, qsc)
        suffix[h] = rest
        suffix_low = rest.astype(BF16)
        scores = jnp.where(causal, dot_nt(qsc, k), 0.0).astype(BF16)
        adj_scores = jnp.where(causal, dot_nt(d, v), 0.0).astype(BF16)
        a_ref[h] = (dot_nn(qsc, state_low) + dot_nn(scores, v)).astype(a_ref.dtype)
        qg_ref[h] = ((dot_nt(d, state_low) + dot_nn(adj_scores, k)) * factor).astype(qg_ref.dtype)
        kg_ref[h] = (dot_nn(v, suffix_low) + dot_tn(adj_scores, qsc)).astype(kg_ref.dtype)
        vg_ref[h] = (dot_nt(k, suffix_low) + dot_tn(scores, d)).astype(vg_ref.dtype)


def exclusive_scan(total, axis, count, reverse):
    carried = jnp.zeros_like(total)
    acc = jnp.zeros_like(total)
    for hop in range(count - 1):
        pair = (count - 1 - hop, count - 2 - hop) if reverse else (hop, hop + 1)
        got = lax.ppermute(carried + total, axis, perm=[pair])
        acc = acc + got
        carried = got
    return acc


def per_device(queries, key_rows, value_rows, out_adjoint, seq_count):
    tok_dev, heads, head_dim = queries.shape
    span = SPAN
    blocks = tok_dev // span
    offset = lax.axis_index("seq") * tok_dev
    position = offset + jnp.arange(tok_dev, dtype=jnp.int32)
    factor = lax.rsqrt(jnp.float32(head_dim) * (position + 1).astype(jnp.float32))[:, None]
    scaled = (queries.astype(F32) * factor[:, :, None]).astype(BF16)
    qh, kh, vh, dh = (jnp.transpose(x, (1, 0, 2)) for x in (scaled, key_rows, value_rows, out_adjoint))

    width = 8 if heads % 8 == 0 and heads > 8 else heads
    groups = heads // width
    state_shape = jax.ShapeDtypeStruct((heads, head_dim, head_dim), F32)
    rows = pl.BlockSpec((width, tok_dev, head_dim), lambda g: (g, 0, 0))
    group_state = pl.BlockSpec((width, head_dim, head_dim), lambda g: (g, 0, 0))
    kv_total, adj_total = pl.pallas_call(
        functools.partial(totals_kernel, width),
        grid=(groups,),
        in_specs=[rows] * 4,
        out_specs=[group_state, group_state],
        out_shape=[state_shape, state_shape],
    )(qh, kh, vh, dh)

    fac = pl.BlockSpec((span, 1), lambda c: (c, 0))
    peers = lax.psum(1, ("head", "sub"))
    tok_out = tok_dev // peers
    split_out = tok_out % span == 0
    per_peer = tok_out // span
    attended = None
    grads = []
    for g in range(groups):
        sel = slice(g * width, (g + 1) * width)
        before = exclusive_scan(kv_total[sel], "seq", seq_count, False)
        rest = exclusive_scan(adj_total[sel], "seq", seq_count, True) + adj_total[sel]
        gtile = pl.BlockSpec((width, span, head_dim), lambda c, g=g: (g, c, 0))
        gwhole = pl.BlockSpec((width, head_dim, head_dim), lambda c: (0, 0, 0))
        if split_out:
            otile = pl.BlockSpec(
                (None, width, span, head_dim), lambda c: (c // per_peer, 0, c % per_peer, 0)
            )
            grad_shape = jax.ShapeDtypeStruct((peers, width, tok_out, head_dim), BF16)
        else:
            otile = pl.BlockSpec((width, span, head_dim), lambda c: (0, c, 0))
            grad_shape = jax.ShapeDtypeStruct((width, tok_dev, head_dim), BF16)
        args = [qh, kh, vh, dh, factor, before, rest]
        specs = [gtile] * 4 + [fac, gwhole, gwhole]
        aliases = {}
        if attended is not None:
            args.append(attended)
            specs.append(pl.BlockSpec(memory_space=pl.ANY))
            aliases = {7: 0}
        outs = pl.pallas_call(
            functools.partial(main_kernel, width, attended is not None),
            grid=(blocks,),
            in_specs=specs,
            out_specs=[gtile] + [otile] * 3,
            out_shape=[jax.ShapeDtypeStruct((heads, tok_dev, head_dim), BF16)] + [grad_shape] * 3,
            scratch_shapes=[pltpu.VMEM((width, head_dim, head_dim), F32)] * 2,
            input_output_aliases=aliases,
            compiler_params=pltpu.CompilerParams(dimension_semantics=("arbitrary",)),
        )(*args)
        attended = outs[0]
        axis = 0 if split_out else 1
        grads.append([
            lax.all_to_all(x, ("head", "sub"), split_axis=axis, concat_axis=0, tiled=True)
            for x in outs[1:]
        ])
    outs = tuple(
        jnp.transpose(
            jnp.stack([grads[g][i].reshape(peers, width, tok_out, head_dim) for g in range(groups)], 1)
            .reshape(heads * peers, tok_out, head_dim),
            (1, 0, 2),
        )
        for i in range(3)
    )
    return (jnp.transpose(attended, (1, 0, 2)),) + outs


def solution(mesh):
    seq_count = mesh.shape["seq"]
    spec_in = P(("grp", "seq"), ("head", "sub"), None)
    spec_grad = P(("grp", "seq", "head", "sub"), None, None)
    return jax.shard_map(
        lambda *a: per_device(*a, seq_count),
        mesh=mesh,
        in_specs=(spec_in,) * 4,
        out_specs=(spec_in, spec_grad, spec_grad, spec_grad),
        check_vma=False,
    )
```

```python
import functools

import jax
import jax.numpy as jnp
from jax import lax
from jax.experimental import pallas as pl
from jax.experimental.pallas import tpu as pltpu
from jax.sharding import PartitionSpec as P

SPAN = 64
F32 = jnp.float32
BF16 = jnp.bfloat16


def dot_nn(a, b):
    return jnp.dot(a, b, preferred_element_type=F32)


def dot_nt(a, b):
    return lax.dot_general(a, b, (((1,), (1,)), ((), ())), preferred_element_type=F32)


def dot_tn(a, b):
    return lax.dot_general(a, b, (((0,), (0,)), ((), ())), preferred_element_type=F32)


def totals_kernel(heads, q_ref, k_ref, v_ref, d_ref, kv_ref, adj_ref):
    for h in range(heads):
        kv_ref[h] = dot_tn(k_ref[h], v_ref[h])
        adj_ref[h] = dot_tn(d_ref[h], q_ref[h])


def intra_kernel(heads, q_ref, k_ref, v_ref, d_ref, a_ref, qg_ref, kg_ref, vg_ref):
    span = q_ref.shape[1]
    row = lax.broadcasted_iota(jnp.int32, (span, span), 0)
    col = lax.broadcasted_iota(jnp.int32, (span, span), 1)
    causal = row >= col
    for h in range(heads):
        qsc = q_ref[h]
        k = k_ref[h]
        v = v_ref[h]
        d = d_ref[h]
        scores = jnp.where(causal, dot_nt(qsc, k), 0.0).astype(BF16)
        adj_scores = jnp.where(causal, dot_nt(d, v), 0.0).astype(BF16)
        a_ref[h] = dot_nn(scores, v)
        qg_ref[h] = dot_nn(adj_scores, k)
        kg_ref[h] = dot_tn(adj_scores, qsc)
        vg_ref[h] = dot_tn(scores, d)


def main_kernel(heads, aliased, q_ref, k_ref, v_ref, d_ref, f_ref, before_ref, rest_ref,
                ai_ref, qgi_ref, kgi_ref, vgi_ref, *refs):
    if aliased:
        refs = refs[1:]
    a_ref, qg_ref, kg_ref, vg_ref, state, suffix = refs

    @pl.when(pl.program_id(0) == 0)
    def _():
        state[...] = before_ref[...]
        suffix[...] = rest_ref[...]

    factor = f_ref[...]
    for h in range(heads):
        qsc = q_ref[h]
        k = k_ref[h]
        v = v_ref[h]
        d = d_ref[h]
        prev = state[h]
        state_low = prev.astype(BF16)
        state[h] = prev + dot_tn(k, v)
        rest = suffix[h] - dot_tn(d, qsc)
        suffix[h] = rest
        suffix_low = rest.astype(BF16)
        a_ref[h] = (dot_nn(qsc, state_low) + ai_ref[h]).astype(a_ref.dtype)
        qg_ref[h] = ((dot_nt(d, state_low) + qgi_ref[h]) * factor).astype(qg_ref.dtype)
        kg_ref[h] = (dot_nn(v, suffix_low) + kgi_ref[h]).astype(kg_ref.dtype)
        vg_ref[h] = (dot_nt(k, suffix_low) + vgi_ref[h]).astype(vg_ref.dtype)


def exclusive_scan(total, axis, count, reverse):
    carried = jnp.zeros_like(total)
    acc = jnp.zeros_like(total)
    for hop in range(count - 1):
        pair = (count - 1 - hop, count - 2 - hop) if reverse else (hop, hop + 1)
        got = lax.ppermute(carried + total, axis, perm=[pair])
        acc = acc + got
        carried = got
    return acc


def per_device(queries, key_rows, value_rows, out_adjoint, seq_count):
    tok_dev, heads, head_dim = queries.shape
    span = SPAN
    blocks = tok_dev // span
    offset = lax.axis_index("seq") * tok_dev
    position = offset + jnp.arange(tok_dev, dtype=jnp.int32)
    factor = lax.rsqrt(jnp.float32(head_dim) * (position + 1).astype(jnp.float32))[:, None]
    scaled = (queries.astype(F32) * factor[:, :, None]).astype(BF16)
    qh, kh, vh, dh = (jnp.transpose(x, (1, 0, 2)) for x in (scaled, key_rows, value_rows, out_adjoint))

    width = 8 if heads % 8 == 0 and heads > 8 else heads
    groups = heads // width
    state_shape = jax.ShapeDtypeStruct((heads, head_dim, head_dim), F32)
    rows = pl.BlockSpec((width, tok_dev, head_dim), lambda g: (g, 0, 0))
    group_state = pl.BlockSpec((width, head_dim, head_dim), lambda g: (g, 0, 0))
    kv_total, adj_total = pl.pallas_call(
        functools.partial(totals_kernel, width),
        grid=(groups,),
        in_specs=[rows] * 4,
        out_specs=[group_state, group_state],
        out_shape=[state_shape, state_shape],
    )(qh, kh, vh, dh)

    all_tile = pl.BlockSpec((heads, span, head_dim), lambda c: (0, c, 0))
    part_shape = jax.ShapeDtypeStruct((heads, tok_dev, head_dim), F32)
    intra = pl.pallas_call(
        functools.partial(intra_kernel, heads),
        grid=(blocks,),
        in_specs=[all_tile] * 4,
        out_specs=[all_tile] * 4,
        out_shape=[part_shape] * 4,
        cost_estimate=pl.CostEstimate(
            flops=12 * heads * tok_dev * span * head_dim,
            transcendentals=0,
            bytes_accessed=24 * heads * tok_dev * head_dim,
        ),
    )(qh, kh, vh, dh)

    fac = pl.BlockSpec((span, 1), lambda c: (c, 0))
    peers = lax.psum(1, ("head", "sub"))
    tok_out = tok_dev // peers
    split_out = tok_out % span == 0
    per_peer = tok_out // span
    attended = None
    grads = []
    for g in range(groups):
        sel = slice(g * width, (g + 1) * width)
        before = exclusive_scan(kv_total[sel], "seq", seq_count, False)
        rest = exclusive_scan(adj_total[sel], "seq", seq_count, True) + adj_total[sel]
        gtile = pl.BlockSpec((width, span, head_dim), lambda c, g=g: (g, c, 0))
        gwhole = pl.BlockSpec((width, head_dim, head_dim), lambda c: (0, 0, 0))
        if split_out:
            otile = pl.BlockSpec(
                (None, width, span, head_dim), lambda c: (c // per_peer, 0, c % per_peer, 0)
            )
            grad_shape = jax.ShapeDtypeStruct((peers, width, tok_out, head_dim), BF16)
        else:
            otile = pl.BlockSpec((width, span, head_dim), lambda c: (0, c, 0))
            grad_shape = jax.ShapeDtypeStruct((width, tok_dev, head_dim), BF16)
        args = [qh, kh, vh, dh, factor, before, rest] + list(intra)
        specs = [gtile] * 4 + [fac, gwhole, gwhole] + [gtile] * 4
        aliases = {}
        if attended is not None:
            args.append(attended)
            specs.append(pl.BlockSpec(memory_space=pl.ANY))
            aliases = {11: 0}
        outs = pl.pallas_call(
            functools.partial(main_kernel, width, attended is not None),
            grid=(blocks,),
            in_specs=specs,
            out_specs=[gtile] + [otile] * 3,
            out_shape=[jax.ShapeDtypeStruct((heads, tok_dev, head_dim), BF16)] + [grad_shape] * 3,
            scratch_shapes=[pltpu.VMEM((width, head_dim, head_dim), F32)] * 2,
            input_output_aliases=aliases,
            compiler_params=pltpu.CompilerParams(dimension_semantics=("arbitrary",)),
        )(*args)
        attended = outs[0]
        axis = 0 if split_out else 1
        grads.append([
            lax.all_to_all(x, ("head", "sub"), split_axis=axis, concat_axis=0, tiled=True)
            for x in outs[1:]
        ])
    outs = tuple(
        jnp.transpose(
            jnp.stack([grads[g][i].reshape(peers, width, tok_out, head_dim) for g in range(groups)], 1)
            .reshape(heads * peers, tok_out, head_dim),
            (1, 0, 2),
        )
        for i in range(3)
    )
    return (jnp.transpose(attended, (1, 0, 2)),) + outs


def solution(mesh):
    seq_count = mesh.shape["seq"]
    spec_in = P(("grp", "seq"), ("head", "sub"), None)
    spec_grad = P(("grp", "seq", "head", "sub"), None, None)
    return jax.shard_map(
        lambda *a: per_device(*a, seq_count),
        mesh=mesh,
        in_specs=(spec_in,) * 4,
        out_specs=(spec_in, spec_grad, spec_grad, spec_grad),
        check_vma=False,
    )
```

```python
import functools

import jax
import jax.numpy as jnp
from jax import lax
from jax.experimental import pallas as pl
from jax.experimental.pallas import tpu as pltpu
from jax.sharding import PartitionSpec as P

SPAN = 64
F32 = jnp.float32
BF16 = jnp.bfloat16


def dot_nn(a, b):
    return jnp.dot(a, b, preferred_element_type=F32)


def dot_nt(a, b):
    return lax.dot_general(a, b, (((1,), (1,)), ((), ())), preferred_element_type=F32)


def dot_tn(a, b):
    return lax.dot_general(a, b, (((0,), (0,)), ((), ())), preferred_element_type=F32)


def totals_kernel(heads, q_ref, k_ref, v_ref, d_ref, kv_ref, adj_ref):
    for h in range(heads):
        kv_ref[h] = dot_tn(k_ref[h], v_ref[h])
        adj_ref[h] = dot_tn(d_ref[h], q_ref[h])


def intra_kernel(heads, q_ref, k_ref, v_ref, d_ref, a_ref, qg_ref, kg_ref, vg_ref):
    span = q_ref.shape[1]
    row = lax.broadcasted_iota(jnp.int32, (span, span), 0)
    col = lax.broadcasted_iota(jnp.int32, (span, span), 1)
    causal = row >= col
    for h in range(heads):
        qsc = q_ref[h]
        k = k_ref[h]
        v = v_ref[h]
        d = d_ref[h]
        scores = jnp.where(causal, dot_nt(qsc, k), 0.0).astype(BF16)
        adj_scores = jnp.where(causal, dot_nt(d, v), 0.0).astype(BF16)
        a_ref[h] = dot_nn(scores, v)
        qg_ref[h] = dot_nn(adj_scores, k)
        kg_ref[h] = dot_tn(adj_scores, qsc)
        vg_ref[h] = dot_tn(scores, d)


def main_kernel(heads, aliased, q_ref, k_ref, v_ref, d_ref, f_ref, before_ref, rest_ref,
                ai_ref, qgi_ref, kgi_ref, vgi_ref, *refs):
    if aliased:
        refs = refs[1:]
    a_ref, qg_ref, kg_ref, vg_ref, state, suffix = refs

    @pl.when(pl.program_id(0) == 0)
    def _():
        state[...] = before_ref[...]
        suffix[...] = rest_ref[...]

    factor = f_ref[...]
    for h in range(heads):
        qsc = q_ref[h]
        k = k_ref[h]
        v = v_ref[h]
        d = d_ref[h]
        prev = state[h]
        state_low = prev.astype(BF16)
        state[h] = prev + dot_tn(k, v)
        rest = suffix[h] - dot_tn(d, qsc)
        suffix[h] = rest
        suffix_low = rest.astype(BF16)
        a_ref[h] = (dot_nn(qsc, state_low) + ai_ref[h]).astype(a_ref.dtype)
        qg_ref[h] = ((dot_nt(d, state_low) + qgi_ref[h]) * factor).astype(qg_ref.dtype)
        kg_ref[h] = (dot_nn(v, suffix_low) + kgi_ref[h]).astype(kg_ref.dtype)
        vg_ref[h] = (dot_nt(k, suffix_low) + vgi_ref[h]).astype(vg_ref.dtype)


def exclusive_scan(total, axis, count, reverse):
    carried = jnp.zeros_like(total)
    acc = jnp.zeros_like(total)
    for hop in range(count - 1):
        pair = (count - 1 - hop, count - 2 - hop) if reverse else (hop, hop + 1)
        got = lax.ppermute(carried + total, axis, perm=[pair])
        acc = acc + got
        carried = got
    return acc


def per_device(queries, key_rows, value_rows, out_adjoint, seq_count):
    tok_dev, heads, head_dim = queries.shape
    span = SPAN
    blocks = tok_dev // span
    offset = lax.axis_index("seq") * tok_dev
    position = offset + jnp.arange(tok_dev, dtype=jnp.int32)
    factor = lax.rsqrt(jnp.float32(head_dim) * (position + 1).astype(jnp.float32))[:, None]
    scaled = (queries.astype(F32) * factor[:, :, None]).astype(BF16)
    qh, kh, vh, dh = (jnp.transpose(x, (1, 0, 2)) for x in (scaled, key_rows, value_rows, out_adjoint))

    width = 8 if heads % 8 == 0 and heads > 8 else heads
    groups = heads // width
    state_shape = jax.ShapeDtypeStruct((heads, head_dim, head_dim), F32)
    rows = pl.BlockSpec((width, tok_dev, head_dim), lambda g: (g, 0, 0))
    group_state = pl.BlockSpec((width, head_dim, head_dim), lambda g: (g, 0, 0))
    kv_total, adj_total = pl.pallas_call(
        functools.partial(totals_kernel, width),
        grid=(groups,),
        in_specs=[rows] * 4,
        out_specs=[group_state, group_state],
        out_shape=[state_shape, state_shape],
    )(qh, kh, vh, dh)

    def intra_part(g):
        tile = pl.BlockSpec((width, span, head_dim), lambda c: (g, c, 0))
        out = pl.BlockSpec((width, span, head_dim), lambda c: (0, c, 0))
        part_shape = jax.ShapeDtypeStruct((width, tok_dev, head_dim), F32)
        return pl.pallas_call(
            functools.partial(intra_kernel, width),
            grid=(blocks,),
            in_specs=[tile] * 4,
            out_specs=[out] * 4,
            out_shape=[part_shape] * 4,
            cost_estimate=pl.CostEstimate(
                flops=12 * width * tok_dev * span * head_dim,
                transcendentals=0,
                bytes_accessed=24 * width * tok_dev * head_dim,
            ),
        )(qh, kh, vh, dh)

    intra = [intra_part(g) for g in range(groups)]

    fac = pl.BlockSpec((span, 1), lambda c: (c, 0))
    peers = lax.psum(1, ("head", "sub"))
    tok_out = tok_dev // peers
    split_out = tok_out % span == 0
    per_peer = tok_out // span
    attended = None
    grads = []
    for g in range(groups):
        sel = slice(g * width, (g + 1) * width)
        before = exclusive_scan(kv_total[sel], "seq", seq_count, False)
        rest = exclusive_scan(adj_total[sel], "seq", seq_count, True) + adj_total[sel]
        gtile = pl.BlockSpec((width, span, head_dim), lambda c, g=g: (g, c, 0))
        gwhole = pl.BlockSpec((width, head_dim, head_dim), lambda c: (0, 0, 0))
        otile_f32 = pl.BlockSpec((width, span, head_dim), lambda c: (0, c, 0))
        if split_out:
            otile = pl.BlockSpec(
                (None, width, span, head_dim), lambda c: (c // per_peer, 0, c % per_peer, 0)
            )
            grad_shape = jax.ShapeDtypeStruct((peers, width, tok_out, head_dim), BF16)
        else:
            otile = pl.BlockSpec((width, span, head_dim), lambda c: (0, c, 0))
            grad_shape = jax.ShapeDtypeStruct((width, tok_dev, head_dim), BF16)
        args = [qh, kh, vh, dh, factor, before, rest] + list(intra[g])
        specs = [gtile] * 4 + [fac, gwhole, gwhole] + [otile_f32] * 4
        aliases = {}
        if attended is not None:
            args.append(attended)
            specs.append(pl.BlockSpec(memory_space=pl.ANY))
            aliases = {11: 0}
        outs = pl.pallas_call(
            functools.partial(main_kernel, width, attended is not None),
            grid=(blocks,),
            in_specs=specs,
            out_specs=[gtile] + [otile] * 3,
            out_shape=[jax.ShapeDtypeStruct((heads, tok_dev, head_dim), BF16)] + [grad_shape] * 3,
            scratch_shapes=[pltpu.VMEM((width, head_dim, head_dim), F32)] * 2,
            input_output_aliases=aliases,
            compiler_params=pltpu.CompilerParams(dimension_semantics=("arbitrary",)),
        )(*args)
        attended = outs[0]
        axis = 0 if split_out else 1
        grads.append([
            lax.all_to_all(x, ("head", "sub"), split_axis=axis, concat_axis=0, tiled=True)
            for x in outs[1:]
        ])
    outs = tuple(
        jnp.transpose(
            jnp.stack([grads[g][i].reshape(peers, width, tok_out, head_dim) for g in range(groups)], 1)
            .reshape(heads * peers, tok_out, head_dim),
            (1, 0, 2),
        )
        for i in range(3)
    )
    return (jnp.transpose(attended, (1, 0, 2)),) + outs


def solution(mesh):
    seq_count = mesh.shape["seq"]
    spec_in = P(("grp", "seq"), ("head", "sub"), None)
    spec_grad = P(("grp", "seq", "head", "sub"), None, None)
    return jax.shard_map(
        lambda *a: per_device(*a, seq_count),
        mesh=mesh,
        in_specs=(spec_in,) * 4,
        out_specs=(spec_in, spec_grad, spec_grad, spec_grad),
        check_vma=False,
    )
```

```python
import functools

import jax
import jax.numpy as jnp
from jax import lax
from jax.experimental import pallas as pl
from jax.experimental.pallas import tpu as pltpu
from jax.sharding import PartitionSpec as P

SPAN = 64
F32 = jnp.float32
BF16 = jnp.bfloat16


def dot_nn(a, b):
    return jnp.dot(a, b, preferred_element_type=F32)


def dot_nt(a, b):
    return lax.dot_general(a, b, (((1,), (1,)), ((), ())), preferred_element_type=F32)


def dot_tn(a, b):
    return lax.dot_general(a, b, (((0,), (0,)), ((), ())), preferred_element_type=F32)


def totals_kernel(heads, q_ref, k_ref, v_ref, d_ref, kv_ref, adj_ref):
    for h in range(heads):
        kv_ref[h] = dot_tn(k_ref[h], v_ref[h])
        adj_ref[h] = dot_tn(d_ref[h], q_ref[h])


def main_kernel(heads, aliased, q_ref, k_ref, v_ref, d_ref, f_ref, before_ref, rest_ref, *refs):
    if aliased:
        refs = refs[1:]
    a_ref, qg_ref, kg_ref, vg_ref, state, suffix = refs

    @pl.when(pl.program_id(0) == 0)
    def _():
        state[...] = before_ref[...]
        suffix[...] = rest_ref[...]

    factor = f_ref[...]
    span = factor.shape[0]
    row = lax.broadcasted_iota(jnp.int32, (span, span), 0)
    col = lax.broadcasted_iota(jnp.int32, (span, span), 1)
    causal = row >= col
    for h in range(heads):
        qsc = q_ref[h]
        k = k_ref[h]
        v = v_ref[h]
        d = d_ref[h]
        prev = state[h]
        state_low = prev.astype(BF16)
        state[h] = prev + dot_tn(k, v)
        rest = suffix[h] - dot_tn(d, qsc)
        suffix[h] = rest
        suffix_low = rest.astype(BF16)
        scores = jnp.where(causal, dot_nt(qsc, k), 0.0).astype(BF16)
        adj_scores = jnp.where(causal, dot_nt(d, v), 0.0).astype(BF16)
        a_ref[h] = (dot_nn(qsc, state_low) + dot_nn(scores, v)).astype(a_ref.dtype)
        qg_ref[h] = ((dot_nt(d, state_low) + dot_nn(adj_scores, k)) * factor).astype(qg_ref.dtype)
        kg_ref[h] = (dot_nn(v, suffix_low) + dot_tn(adj_scores, qsc)).astype(kg_ref.dtype)
        vg_ref[h] = (dot_nt(k, suffix_low) + dot_tn(scores, d)).astype(vg_ref.dtype)


def exclusive_scan(total, axis, count, reverse):
    carried = jnp.zeros_like(total)
    acc = jnp.zeros_like(total)
    hops = []
    for hop in range(count - 1):
        pair = (count - 1 - hop, count - 2 - hop) if reverse else (hop, hop + 1)
        got = lax.ppermute(carried + total, axis, perm=[pair])
        acc = acc + got
        carried = got
        hops.append(got)
    return acc, hops


def per_device(queries, key_rows, value_rows, out_adjoint, seq_count):
    tok_dev, heads, head_dim = queries.shape
    span = SPAN
    blocks = tok_dev // span
    offset = lax.axis_index("seq") * tok_dev
    position = offset + jnp.arange(tok_dev, dtype=jnp.int32)
    factor = lax.rsqrt(jnp.float32(head_dim) * (position + 1).astype(jnp.float32))[:, None]
    scaled = (queries.astype(F32) * factor[:, :, None]).astype(BF16)
    qh, kh, vh, dh = (jnp.transpose(x, (1, 0, 2)) for x in (scaled, key_rows, value_rows, out_adjoint))

    width = 8 if heads % 8 == 0 and heads > 8 else heads
    groups = heads // width
    state_shape = jax.ShapeDtypeStruct((heads, head_dim, head_dim), F32)
    rows = pl.BlockSpec((width, tok_dev, head_dim), lambda g: (g, 0, 0))
    group_state = pl.BlockSpec((width, head_dim, head_dim), lambda g: (g, 0, 0))
    kv_total, adj_total = pl.pallas_call(
        functools.partial(totals_kernel, width),
        grid=(groups,),
        in_specs=[rows] * 4,
        out_specs=[group_state, group_state],
        out_shape=[state_shape, state_shape],
    )(qh, kh, vh, dh)

    fac = pl.BlockSpec((span, 1), lambda c: (c, 0))
    peers = lax.psum(1, ("head", "sub"))
    tok_out = tok_dev // peers
    split_out = tok_out % span == 0
    per_peer = tok_out // span
    attended = None
    grads = []
    chains = []
    for g in range(groups):
        sel = slice(g * width, (g + 1) * width)
        before, before_hops = exclusive_scan(kv_total[sel], "seq", seq_count, False)
        after, after_hops = exclusive_scan(adj_total[sel], "seq", seq_count, True)
        chains.append([before, after + adj_total[sel], before_hops, after_hops])
    for g in range(groups - 1):
        if seq_count >= 3:
            nxt = chains[g + 1]
            chains[g][0], chains[g][1], _, _ = lax.optimization_barrier(
                (chains[g][0], chains[g][1], nxt[2][seq_count - 3], nxt[3][seq_count - 3])
            )
    for g in range(groups):
        before, rest = chains[g][0], chains[g][1]
        gtile = pl.BlockSpec((width, span, head_dim), lambda c, g=g: (g, c, 0))
        gwhole = pl.BlockSpec((width, head_dim, head_dim), lambda c: (0, 0, 0))
        if split_out:
            otile = pl.BlockSpec(
                (None, width, span, head_dim), lambda c: (c // per_peer, 0, c % per_peer, 0)
            )
            grad_shape = jax.ShapeDtypeStruct((peers, width, tok_out, head_dim), BF16)
        else:
            otile = pl.BlockSpec((width, span, head_dim), lambda c: (0, c, 0))
            grad_shape = jax.ShapeDtypeStruct((width, tok_dev, head_dim), BF16)
        args = [qh, kh, vh, dh, factor, before, rest]
        specs = [gtile] * 4 + [fac, gwhole, gwhole]
        aliases = {}
        if attended is not None:
            args.append(attended)
            specs.append(pl.BlockSpec(memory_space=pl.ANY))
            aliases = {7: 0}
        outs = pl.pallas_call(
            functools.partial(main_kernel, width, attended is not None),
            grid=(blocks,),
            in_specs=specs,
            out_specs=[gtile] + [otile] * 3,
            out_shape=[jax.ShapeDtypeStruct((heads, tok_dev, head_dim), BF16)] + [grad_shape] * 3,
            scratch_shapes=[pltpu.VMEM((width, head_dim, head_dim), F32)] * 2,
            input_output_aliases=aliases,
            compiler_params=pltpu.CompilerParams(dimension_semantics=("arbitrary",)),
        )(*args)
        attended = outs[0]
        axis = 0 if split_out else 1
        grads.append([
            lax.all_to_all(x, ("head", "sub"), split_axis=axis, concat_axis=0, tiled=True)
            for x in outs[1:]
        ])
    outs = tuple(
        jnp.transpose(
            jnp.stack([grads[g][i].reshape(peers, width, tok_out, head_dim) for g in range(groups)], 1)
            .reshape(heads * peers, tok_out, head_dim),
            (1, 0, 2),
        )
        for i in range(3)
    )
    return (jnp.transpose(attended, (1, 0, 2)),) + outs


def solution(mesh):
    seq_count = mesh.shape["seq"]
    spec_in = P(("grp", "seq"), ("head", "sub"), None)
    spec_grad = P(("grp", "seq", "head", "sub"), None, None)
    return jax.shard_map(
        lambda *a: per_device(*a, seq_count),
        mesh=mesh,
        in_specs=(spec_in,) * 4,
        out_specs=(spec_in, spec_grad, spec_grad, spec_grad),
        check_vma=False,
    )
```

```python
import functools

import jax
import jax.numpy as jnp
from jax import lax
from jax.experimental import pallas as pl
from jax.experimental.pallas import tpu as pltpu
from jax.sharding import PartitionSpec as P

SPAN = 64
F32 = jnp.float32
BF16 = jnp.bfloat16


def dot_nn(a, b):
    return jnp.dot(a, b, preferred_element_type=F32)


def dot_nt(a, b):
    return lax.dot_general(a, b, (((1,), (1,)), ((), ())), preferred_element_type=F32)


def dot_tn(a, b):
    return lax.dot_general(a, b, (((0,), (0,)), ((), ())), preferred_element_type=F32)


def totals_kernel(heads, q_ref, k_ref, v_ref, d_ref, kv_ref, adj_ref):
    for h in range(heads):
        kv_ref[h] = dot_tn(k_ref[h], v_ref[h])
        adj_ref[h] = dot_tn(d_ref[h], q_ref[h])


def main_kernel(heads, aliased, q_ref, k_ref, v_ref, d_ref, f_ref, before_ref, rest_ref, *refs):
    if aliased:
        refs = refs[1:]
    a_ref, qg_ref, kg_ref, vg_ref, state, suffix = refs

    @pl.when(pl.program_id(0) == 0)
    def _():
        state[...] = before_ref[...]
        suffix[...] = rest_ref[...]

    factor = f_ref[...]
    span = factor.shape[0]
    row = lax.broadcasted_iota(jnp.int32, (span, span), 0)
    col = lax.broadcasted_iota(jnp.int32, (span, span), 1)
    causal = row >= col
    for h in range(heads):
        qsc = q_ref[h]
        k = k_ref[h]
        v = v_ref[h]
        d = d_ref[h]
        prev = state[h]
        state_low = prev.astype(BF16)
        state[h] = prev + dot_tn(k, v)
        rest = suffix[h] - dot_tn(d, qsc)
        suffix[h] = rest
        suffix_low = rest.astype(BF16)
        scores = jnp.where(causal, dot_nt(qsc, k), 0.0).astype(BF16)
        adj_scores = jnp.where(causal, dot_nt(d, v), 0.0).astype(BF16)
        a_ref[h] = (dot_nn(qsc, state_low) + dot_nn(scores, v)).astype(a_ref.dtype)
        qg_ref[h] = ((dot_nt(d, state_low) + dot_nn(adj_scores, k)) * factor).astype(qg_ref.dtype)
        kg_ref[h] = (dot_nn(v, suffix_low) + dot_tn(adj_scores, qsc)).astype(kg_ref.dtype)
        vg_ref[h] = (dot_nt(k, suffix_low) + dot_tn(scores, d)).astype(vg_ref.dtype)


def exclusive_scan(total, axis, count, reverse):
    carried = jnp.zeros_like(total)
    acc = jnp.zeros_like(total)
    hops = []
    for hop in range(count - 1):
        pair = (count - 1 - hop, count - 2 - hop) if reverse else (hop, hop + 1)
        got = lax.ppermute(carried + total, axis, perm=[pair])
        acc = acc + got
        carried = got
        hops.append(got)
    return acc, hops


def per_device(queries, key_rows, value_rows, out_adjoint, seq_count):
    tok_dev, heads, head_dim = queries.shape
    span = SPAN
    blocks = tok_dev // span
    offset = lax.axis_index("seq") * tok_dev
    position = offset + jnp.arange(tok_dev, dtype=jnp.int32)
    factor = lax.rsqrt(jnp.float32(head_dim) * (position + 1).astype(jnp.float32))[:, None]
    scaled = (queries.astype(F32) * factor[:, :, None]).astype(BF16)
    qh, kh, vh, dh = (jnp.transpose(x, (1, 0, 2)) for x in (scaled, key_rows, value_rows, out_adjoint))

    width = 8 if heads % 8 == 0 and heads > 8 else heads
    groups = heads // width
    state_shape = jax.ShapeDtypeStruct((heads, head_dim, head_dim), F32)
    rows = pl.BlockSpec((width, tok_dev, head_dim), lambda g: (g, 0, 0))
    group_state = pl.BlockSpec((width, head_dim, head_dim), lambda g: (g, 0, 0))
    kv_total, adj_total = pl.pallas_call(
        functools.partial(totals_kernel, width),
        grid=(groups,),
        in_specs=[rows] * 4,
        out_specs=[group_state, group_state],
        out_shape=[state_shape, state_shape],
    )(qh, kh, vh, dh)

    fac = pl.BlockSpec((span, 1), lambda c: (c, 0))
    peers = lax.psum(1, ("head", "sub"))
    tok_out = tok_dev // peers
    split_out = tok_out % span == 0
    per_peer = tok_out // span
    attended = None
    grads = []
    chains = []
    for g in range(groups):
        sel = slice(g * width, (g + 1) * width)
        before, before_hops = exclusive_scan(kv_total[sel], "seq", seq_count, False)
        after, after_hops = exclusive_scan(adj_total[sel], "seq", seq_count, True)
        chains.append([before, after + adj_total[sel], before_hops, after_hops])
    for g in range(groups - 1):
        if seq_count >= 3:
            nxt = chains[g + 1]
            chains[g][0], chains[g][1], _, _ = lax.optimization_barrier(
                (chains[g][0], chains[g][1], nxt[2][seq_count - 3], nxt[3][seq_count - 3])
            )
    for g in range(groups):
        before, rest = chains[g][0], chains[g][1]
        gtile = pl.BlockSpec((width, span, head_dim), lambda c, g=g: (g, c, 0))
        gwhole = pl.BlockSpec((width, head_dim, head_dim), lambda c: (0, 0, 0))
        if split_out:
            otile = pl.BlockSpec(
                (None, width, span, head_dim), lambda c: (c // per_peer, 0, c % per_peer, 0)
            )
            grad_shape = jax.ShapeDtypeStruct((peers, width, tok_out, head_dim), BF16)
        else:
            otile = pl.BlockSpec((width, span, head_dim), lambda c: (0, c, 0))
            grad_shape = jax.ShapeDtypeStruct((width, tok_dev, head_dim), BF16)
        args = [qh, kh, vh, dh, factor, before, rest]
        specs = [gtile] * 4 + [fac, gwhole, gwhole]
        aliases = {}
        if attended is not None:
            args.append(attended)
            specs.append(pl.BlockSpec(memory_space=pl.ANY))
            aliases = {7: 0}
        outs = pl.pallas_call(
            functools.partial(main_kernel, width, attended is not None),
            grid=(blocks,),
            in_specs=specs,
            out_specs=[gtile] + [otile] * 3,
            out_shape=[jax.ShapeDtypeStruct((heads, tok_dev, head_dim), BF16)] + [grad_shape] * 3,
            scratch_shapes=[pltpu.VMEM((width, head_dim, head_dim), F32)] * 2,
            input_output_aliases=aliases,
            compiler_params=pltpu.CompilerParams(dimension_semantics=("arbitrary",)),
        )(*args)
        attended = outs[0]
        grads.append(list(outs[1:]))
    if groups > 1:
        grads[0], _ = lax.optimization_barrier((grads[0], grads[-1]))
    axis = 0 if split_out else 1
    grads = [
        [lax.all_to_all(x, ("head", "sub"), split_axis=axis, concat_axis=0, tiled=True) for x in gr]
        for gr in grads
    ]
    outs = tuple(
        jnp.transpose(
            jnp.stack([grads[g][i].reshape(peers, width, tok_out, head_dim) for g in range(groups)], 1)
            .reshape(heads * peers, tok_out, head_dim),
            (1, 0, 2),
        )
        for i in range(3)
    )
    return (jnp.transpose(attended, (1, 0, 2)),) + outs


def solution(mesh):
    seq_count = mesh.shape["seq"]
    spec_in = P(("grp", "seq"), ("head", "sub"), None)
    spec_grad = P(("grp", "seq", "head", "sub"), None, None)
    return jax.shard_map(
        lambda *a: per_device(*a, seq_count),
        mesh=mesh,
        in_specs=(spec_in,) * 4,
        out_specs=(spec_in, spec_grad, spec_grad, spec_grad),
        check_vma=False,
    )
```

```python
import functools

import jax
import jax.numpy as jnp
from jax import lax
from jax.experimental import pallas as pl
from jax.experimental.pallas import tpu as pltpu
from jax.sharding import PartitionSpec as P

SPAN = 64
F32 = jnp.float32
BF16 = jnp.bfloat16


def dot_nn(a, b):
    return jnp.dot(a, b, preferred_element_type=F32)


def dot_nt(a, b):
    return lax.dot_general(a, b, (((1,), (1,)), ((), ())), preferred_element_type=F32)


def dot_tn(a, b):
    return lax.dot_general(a, b, (((0,), (0,)), ((), ())), preferred_element_type=F32)


def totals_kernel(heads, q_ref, k_ref, v_ref, d_ref, kv_ref, adj_ref):
    for h in range(heads):
        kv_ref[h] = dot_tn(k_ref[h], v_ref[h])
        adj_ref[h] = dot_tn(d_ref[h], q_ref[h])


def main_kernel(heads, aliased, q_ref, k_ref, v_ref, d_ref, f_ref, before_ref, rest_ref, *refs):
    if aliased:
        refs = refs[1:]
    a_ref, g_ref, state, suffix = refs
    qg_ref, kg_ref, vg_ref = g_ref.at[0], g_ref.at[1], g_ref.at[2]

    @pl.when(pl.program_id(0) == 0)
    def _():
        state[...] = before_ref[...]
        suffix[...] = rest_ref[...]

    factor = f_ref[...]
    span = factor.shape[0]
    row = lax.broadcasted_iota(jnp.int32, (span, span), 0)
    col = lax.broadcasted_iota(jnp.int32, (span, span), 1)
    causal = row >= col
    for h in range(heads):
        qsc = q_ref[h]
        k = k_ref[h]
        v = v_ref[h]
        d = d_ref[h]
        prev = state[h]
        state_low = prev.astype(BF16)
        state[h] = prev + dot_tn(k, v)
        rest = suffix[h] - dot_tn(d, qsc)
        suffix[h] = rest
        suffix_low = rest.astype(BF16)
        scores = jnp.where(causal, dot_nt(qsc, k), 0.0).astype(BF16)
        adj_scores = jnp.where(causal, dot_nt(d, v), 0.0).astype(BF16)
        a_ref[h] = (dot_nn(qsc, state_low) + dot_nn(scores, v)).astype(a_ref.dtype)
        qg_ref[h] = ((dot_nt(d, state_low) + dot_nn(adj_scores, k)) * factor).astype(qg_ref.dtype)
        kg_ref[h] = (dot_nn(v, suffix_low) + dot_tn(adj_scores, qsc)).astype(kg_ref.dtype)
        vg_ref[h] = (dot_nt(k, suffix_low) + dot_tn(scores, d)).astype(vg_ref.dtype)


def exclusive_scan(total, axis, count, reverse):
    carried = jnp.zeros_like(total)
    acc = jnp.zeros_like(total)
    for hop in range(count - 1):
        pair = (count - 1 - hop, count - 2 - hop) if reverse else (hop, hop + 1)
        got = lax.ppermute(carried + total, axis, perm=[pair])
        acc = acc + got
        carried = got
    return acc


def per_device(queries, key_rows, value_rows, out_adjoint, seq_count):
    tok_dev, heads, head_dim = queries.shape
    span = SPAN
    blocks = tok_dev // span
    offset = lax.axis_index("seq") * tok_dev
    position = offset + jnp.arange(tok_dev, dtype=jnp.int32)
    factor = lax.rsqrt(jnp.float32(head_dim) * (position + 1).astype(jnp.float32))[:, None]
    scaled = (queries.astype(F32) * factor[:, :, None]).astype(BF16)
    qh, kh, vh, dh = (jnp.transpose(x, (1, 0, 2)) for x in (scaled, key_rows, value_rows, out_adjoint))

    width = 8 if heads % 8 == 0 and heads > 8 else heads
    groups = heads // width
    state_shape = jax.ShapeDtypeStruct((heads, head_dim, head_dim), F32)
    rows = pl.BlockSpec((width, tok_dev, head_dim), lambda g: (g, 0, 0))
    group_state = pl.BlockSpec((width, head_dim, head_dim), lambda g: (g, 0, 0))
    kv_total, adj_total = pl.pallas_call(
        functools.partial(totals_kernel, width),
        grid=(groups,),
        in_specs=[rows] * 4,
        out_specs=[group_state, group_state],
        out_shape=[state_shape, state_shape],
    )(qh, kh, vh, dh)

    fac = pl.BlockSpec((span, 1), lambda c: (c, 0))
    peers = lax.psum(1, ("head", "sub"))
    tok_out = tok_dev // peers
    split_out = tok_out % span == 0
    per_peer = tok_out // span
    attended = None
    grads = []
    for g in range(groups):
        sel = slice(g * width, (g + 1) * width)
        before = exclusive_scan(kv_total[sel], "seq", seq_count, False)
        rest = exclusive_scan(adj_total[sel], "seq", seq_count, True) + adj_total[sel]
        gtile = pl.BlockSpec((width, span, head_dim), lambda c, g=g: (g, c, 0))
        gwhole = pl.BlockSpec((width, head_dim, head_dim), lambda c: (0, 0, 0))
        if split_out:
            otile = pl.BlockSpec(
                (None, 3, width, span, head_dim), lambda c: (c // per_peer, 0, 0, c % per_peer, 0)
            )
            grad_shape = jax.ShapeDtypeStruct((peers, 3, width, tok_out, head_dim), BF16)
        else:
            otile = pl.BlockSpec((3, width, span, head_dim), lambda c: (0, 0, c, 0))
            grad_shape = jax.ShapeDtypeStruct((3, width, tok_dev, head_dim), BF16)
        args = [qh, kh, vh, dh, factor, before, rest]
        specs = [gtile] * 4 + [fac, gwhole, gwhole]
        aliases = {}
        if attended is not None:
            args.append(attended)
            specs.append(pl.BlockSpec(memory_space=pl.ANY))
            aliases = {7: 0}
        outs = pl.pallas_call(
            functools.partial(main_kernel, width, attended is not None),
            grid=(blocks,),
            in_specs=specs,
            out_specs=[gtile, otile],
            out_shape=[jax.ShapeDtypeStruct((heads, tok_dev, head_dim), BF16), grad_shape],
            scratch_shapes=[pltpu.VMEM((width, head_dim, head_dim), F32)] * 2,
            input_output_aliases=aliases,
            compiler_params=pltpu.CompilerParams(dimension_semantics=("arbitrary",)),
        )(*args)
        attended = outs[0]
        axis = 0 if split_out else 2
        grads.append(
            lax.all_to_all(outs[1], ("head", "sub"), split_axis=axis, concat_axis=0, tiled=True)
        )
    if split_out:
        parts = [gr for gr in grads]
    else:
        parts = [gr.reshape(peers, 3, width, tok_out, head_dim) for gr in grads]
    outs = tuple(
        jnp.transpose(
            jnp.stack([p[:, i] for p in parts], 1).reshape(heads * peers, tok_out, head_dim),
            (1, 0, 2),
        )
        for i in range(3)
    )
    return (jnp.transpose(attended, (1, 0, 2)),) + outs


def solution(mesh):
    seq_count = mesh.shape["seq"]
    spec_in = P(("grp", "seq"), ("head", "sub"), None)
    spec_grad = P(("grp", "seq", "head", "sub"), None, None)
    return jax.shard_map(
        lambda *a: per_device(*a, seq_count),
        mesh=mesh,
        in_specs=(spec_in,) * 4,
        out_specs=(spec_in, spec_grad, spec_grad, spec_grad),
        check_vma=False,
    )
```

```python
import functools

import jax
import jax.numpy as jnp
from jax import lax
from jax.experimental import pallas as pl
from jax.experimental.pallas import tpu as pltpu
from jax.sharding import PartitionSpec as P

SPAN = 64
F32 = jnp.float32
BF16 = jnp.bfloat16


def dot_nn(a, b):
    return jnp.dot(a, b, preferred_element_type=F32)


def dot_nt(a, b):
    return lax.dot_general(a, b, (((1,), (1,)), ((), ())), preferred_element_type=F32)


def dot_tn(a, b):
    return lax.dot_general(a, b, (((0,), (0,)), ((), ())), preferred_element_type=F32)


def totals_kernel(heads, q_ref, k_ref, v_ref, d_ref, kv_ref, adj_ref):
    for h in range(heads):
        kv_ref[h] = dot_tn(k_ref[h], v_ref[h])
        adj_ref[h] = dot_tn(d_ref[h], q_ref[h])


def main_kernel(heads, aliased, q_ref, k_ref, v_ref, d_ref, f_ref, before_ref, rest_ref, *refs):
    if aliased:
        refs = refs[1:]
    a_ref, g_ref, state, suffix = refs
    qg_ref, kg_ref, vg_ref = g_ref.at[0], g_ref.at[1], g_ref.at[2]

    @pl.when(pl.program_id(0) == 0)
    def _():
        state[...] = before_ref[...]
        suffix[...] = rest_ref[...]

    factor = f_ref[...]
    span = factor.shape[0]
    row = lax.broadcasted_iota(jnp.int32, (span, span), 0)
    col = lax.broadcasted_iota(jnp.int32, (span, span), 1)
    causal = row >= col
    for h in range(heads):
        qsc = q_ref[h]
        k = k_ref[h]
        v = v_ref[h]
        d = d_ref[h]
        prev = state[h]
        state_low = prev.astype(BF16)
        state[h] = prev + dot_tn(k, v)
        rest = suffix[h] - dot_tn(d, qsc)
        suffix[h] = rest
        suffix_low = rest.astype(BF16)
        scores = jnp.where(causal, dot_nt(qsc, k), 0.0).astype(BF16)
        adj_scores = jnp.where(causal, dot_nt(d, v), 0.0).astype(BF16)
        a_ref[h] = (dot_nn(qsc, state_low) + dot_nn(scores, v)).astype(a_ref.dtype)
        qg_ref[h] = ((dot_nt(d, state_low) + dot_nn(adj_scores, k)) * factor).astype(qg_ref.dtype)
        kg_ref[h] = (dot_nn(v, suffix_low) + dot_tn(adj_scores, qsc)).astype(kg_ref.dtype)
        vg_ref[h] = (dot_nt(k, suffix_low) + dot_tn(scores, d)).astype(vg_ref.dtype)


def exclusive_scan(total, axis, count, reverse):
    carried = jnp.zeros_like(total)
    acc = jnp.zeros_like(total)
    hops = []
    for hop in range(count - 1):
        pair = (count - 1 - hop, count - 2 - hop) if reverse else (hop, hop + 1)
        got = lax.ppermute(carried + total, axis, perm=[pair])
        acc = acc + got
        carried = got
        hops.append(got)
    return acc, hops


def per_device(queries, key_rows, value_rows, out_adjoint, seq_count):
    tok_dev, heads, head_dim = queries.shape
    span = SPAN
    blocks = tok_dev // span
    offset = lax.axis_index("seq") * tok_dev
    position = offset + jnp.arange(tok_dev, dtype=jnp.int32)
    factor = lax.rsqrt(jnp.float32(head_dim) * (position + 1).astype(jnp.float32))[:, None]
    scaled = (queries.astype(F32) * factor[:, :, None]).astype(BF16)
    qh, kh, vh, dh = (jnp.transpose(x, (1, 0, 2)) for x in (scaled, key_rows, value_rows, out_adjoint))

    width = 8 if heads % 8 == 0 and heads > 8 else heads
    groups = heads // width
    state_shape = jax.ShapeDtypeStruct((heads, head_dim, head_dim), F32)
    rows = pl.BlockSpec((width, tok_dev, head_dim), lambda g: (g, 0, 0))
    group_state = pl.BlockSpec((width, head_dim, head_dim), lambda g: (g, 0, 0))
    kv_total, adj_total = pl.pallas_call(
        functools.partial(totals_kernel, width),
        grid=(groups,),
        in_specs=[rows] * 4,
        out_specs=[group_state, group_state],
        out_shape=[state_shape, state_shape],
    )(qh, kh, vh, dh)

    fac = pl.BlockSpec((span, 1), lambda c: (c, 0))
    peers = lax.psum(1, ("head", "sub"))
    tok_out = tok_dev // peers
    split_out = tok_out % span == 0
    per_peer = tok_out // span
    attended = None
    grads = []
    chains = []
    for g in range(groups):
        sel = slice(g * width, (g + 1) * width)
        before, before_hops = exclusive_scan(kv_total[sel], "seq", seq_count, False)
        after, after_hops = exclusive_scan(adj_total[sel], "seq", seq_count, True)
        chains.append([before, after + adj_total[sel], before_hops, after_hops])
    for g in range(groups - 1):
        if seq_count >= 3:
            nxt = chains[g + 1]
            chains[g][0], chains[g][1], _, _ = lax.optimization_barrier(
                (chains[g][0], chains[g][1], nxt[2][seq_count - 3], nxt[3][seq_count - 3])
            )
    for g in range(groups):
        before, rest = chains[g][0], chains[g][1]
        gtile = pl.BlockSpec((width, span, head_dim), lambda c, g=g: (g, c, 0))
        gwhole = pl.BlockSpec((width, head_dim, head_dim), lambda c: (0, 0, 0))
        if split_out:
            otile = pl.BlockSpec(
                (None, 3, width, span, head_dim), lambda c: (c // per_peer, 0, 0, c % per_peer, 0)
            )
            grad_shape = jax.ShapeDtypeStruct((peers, 3, width, tok_out, head_dim), BF16)
        else:
            otile = pl.BlockSpec((3, width, span, head_dim), lambda c: (0, 0, c, 0))
            grad_shape = jax.ShapeDtypeStruct((3, width, tok_dev, head_dim), BF16)
        args = [qh, kh, vh, dh, factor, before, rest]
        specs = [gtile] * 4 + [fac, gwhole, gwhole]
        aliases = {}
        if attended is not None:
            args.append(attended)
            specs.append(pl.BlockSpec(memory_space=pl.ANY))
            aliases = {7: 0}
        outs = pl.pallas_call(
            functools.partial(main_kernel, width, attended is not None),
            grid=(blocks,),
            in_specs=specs,
            out_specs=[gtile, otile],
            out_shape=[jax.ShapeDtypeStruct((heads, tok_dev, head_dim), BF16), grad_shape],
            scratch_shapes=[pltpu.VMEM((width, head_dim, head_dim), F32)] * 2,
            input_output_aliases=aliases,
            compiler_params=pltpu.CompilerParams(dimension_semantics=("arbitrary",)),
        )(*args)
        attended = outs[0]
        axis = 0 if split_out else 2
        grads.append(
            lax.all_to_all(outs[1], ("head", "sub"), split_axis=axis, concat_axis=0, tiled=True)
        )
    if split_out:
        parts = [gr for gr in grads]
    else:
        parts = [gr.reshape(peers, 3, width, tok_out, head_dim) for gr in grads]
    outs = tuple(
        jnp.transpose(
            jnp.stack([p[:, i] for p in parts], 1).reshape(heads * peers, tok_out, head_dim),
            (1, 0, 2),
        )
        for i in range(3)
    )
    return (jnp.transpose(attended, (1, 0, 2)),) + outs


def solution(mesh):
    seq_count = mesh.shape["seq"]
    spec_in = P(("grp", "seq"), ("head", "sub"), None)
    spec_grad = P(("grp", "seq", "head", "sub"), None, None)
    return jax.shard_map(
        lambda *a: per_device(*a, seq_count),
        mesh=mesh,
        in_specs=(spec_in,) * 4,
        out_specs=(spec_in, spec_grad, spec_grad, spec_grad),
        check_vma=False,
    )
```

```python
import functools

import jax
import jax.numpy as jnp
from jax import lax
from jax.experimental import pallas as pl
from jax.experimental.pallas import tpu as pltpu
from jax.sharding import PartitionSpec as P

SPAN = 64
F32 = jnp.float32
BF16 = jnp.bfloat16


def dot_nn(a, b):
    return jnp.dot(a, b, preferred_element_type=F32)


def dot_nt(a, b):
    return lax.dot_general(a, b, (((1,), (1,)), ((), ())), preferred_element_type=F32)


def dot_tn(a, b):
    return lax.dot_general(a, b, (((0,), (0,)), ((), ())), preferred_element_type=F32)


def totals_kernel(heads, q_ref, k_ref, v_ref, d_ref, kv_ref, adj_ref):
    for h in range(heads):
        kv_ref[h] = dot_tn(k_ref[h], v_ref[h])
        adj_ref[h] = dot_tn(d_ref[h], q_ref[h])


def main_kernel(heads, aliased, q_ref, k_ref, v_ref, d_ref, f_ref, before_ref, rest_ref, *refs):
    if aliased:
        refs = refs[1:]
    a_ref, g_ref, state, suffix = refs
    qg_ref, kg_ref, vg_ref = g_ref.at[0], g_ref.at[1], g_ref.at[2]

    @pl.when(pl.program_id(0) == 0)
    def _():
        state[...] = before_ref[...]
        suffix[...] = rest_ref[...]

    factor = f_ref[...]
    span = factor.shape[0]
    row = lax.broadcasted_iota(jnp.int32, (span, span), 0)
    col = lax.broadcasted_iota(jnp.int32, (span, span), 1)
    causal = row >= col
    for h in range(heads):
        qsc = q_ref[h]
        k = k_ref[h]
        v = v_ref[h]
        d = d_ref[h]
        prev = state[h]
        state_low = prev.astype(BF16)
        state[h] = prev + dot_tn(k, v)
        rest = suffix[h] - dot_tn(d, qsc)
        suffix[h] = rest
        suffix_low = rest.astype(BF16)
        scores = jnp.where(causal, dot_nt(qsc, k), 0.0).astype(BF16)
        adj_scores = jnp.where(causal, dot_nt(d, v), 0.0).astype(BF16)
        a_ref[h] = (dot_nn(qsc, state_low) + dot_nn(scores, v)).astype(a_ref.dtype)
        qg_ref[h] = ((dot_nt(d, state_low) + dot_nn(adj_scores, k)) * factor).astype(qg_ref.dtype)
        kg_ref[h] = (dot_nn(v, suffix_low) + dot_tn(adj_scores, qsc)).astype(kg_ref.dtype)
        vg_ref[h] = (dot_nt(k, suffix_low) + dot_tn(scores, d)).astype(vg_ref.dtype)


def exclusive_scan(total, axis, count, reverse):
    carried = jnp.zeros_like(total)
    acc = jnp.zeros_like(total)
    hops = []
    for hop in range(count - 1):
        pair = (count - 1 - hop, count - 2 - hop) if reverse else (hop, hop + 1)
        got = lax.ppermute(carried + total, axis, perm=[pair])
        acc = acc + got
        carried = got
        hops.append(got)
    return acc, hops


def per_device(queries, key_rows, value_rows, out_adjoint, seq_count):
    tok_dev, heads, head_dim = queries.shape
    span = SPAN
    blocks = tok_dev // span
    offset = lax.axis_index("seq") * tok_dev
    position = offset + jnp.arange(tok_dev, dtype=jnp.int32)
    factor = lax.rsqrt(jnp.float32(head_dim) * (position + 1).astype(jnp.float32))[:, None]
    scaled = (queries.astype(F32) * factor[:, :, None]).astype(BF16)
    qh, kh, vh, dh = (jnp.transpose(x, (1, 0, 2)) for x in (scaled, key_rows, value_rows, out_adjoint))

    width = 8 if heads % 8 == 0 and heads > 8 else heads
    groups = heads // width
    state_shape = jax.ShapeDtypeStruct((heads, head_dim, head_dim), F32)
    rows = pl.BlockSpec((width, tok_dev, head_dim), lambda g: (g, 0, 0))
    group_state = pl.BlockSpec((width, head_dim, head_dim), lambda g: (g, 0, 0))
    kv_total, adj_total = pl.pallas_call(
        functools.partial(totals_kernel, width),
        grid=(groups,),
        in_specs=[rows] * 4,
        out_specs=[group_state, group_state],
        out_shape=[state_shape, state_shape],
    )(qh, kh, vh, dh)

    fac = pl.BlockSpec((span, 1), lambda c: (c, 0))
    peers = lax.psum(1, ("head", "sub"))
    tok_out = tok_dev // peers
    split_out = tok_out % span == 0
    per_peer = tok_out // span
    attended = None
    grads = []
    chains = []
    for g in range(groups):
        sel = slice(g * width, (g + 1) * width)
        before, before_hops = exclusive_scan(kv_total[sel], "seq", seq_count, False)
        after, after_hops = exclusive_scan(adj_total[sel], "seq", seq_count, True)
        chains.append([before, after + adj_total[sel], before_hops, after_hops])
    for g in range(groups - 1):
        if seq_count >= 2:
            nxt = chains[g + 1]
            chains[g][0], chains[g][1], _, _ = lax.optimization_barrier(
                (chains[g][0], chains[g][1], nxt[2][seq_count - 2], nxt[3][seq_count - 2])
            )
    for g in range(groups):
        before, rest = chains[g][0], chains[g][1]
        gtile = pl.BlockSpec((width, span, head_dim), lambda c, g=g: (g, c, 0))
        gwhole = pl.BlockSpec((width, head_dim, head_dim), lambda c: (0, 0, 0))
        if split_out:
            otile = pl.BlockSpec(
                (None, 3, width, span, head_dim), lambda c: (c // per_peer, 0, 0, c % per_peer, 0)
            )
            grad_shape = jax.ShapeDtypeStruct((peers, 3, width, tok_out, head_dim), BF16)
        else:
            otile = pl.BlockSpec((3, width, span, head_dim), lambda c: (0, 0, c, 0))
            grad_shape = jax.ShapeDtypeStruct((3, width, tok_dev, head_dim), BF16)
        args = [qh, kh, vh, dh, factor, before, rest]
        specs = [gtile] * 4 + [fac, gwhole, gwhole]
        aliases = {}
        if attended is not None:
            args.append(attended)
            specs.append(pl.BlockSpec(memory_space=pl.ANY))
            aliases = {7: 0}
        outs = pl.pallas_call(
            functools.partial(main_kernel, width, attended is not None),
            grid=(blocks,),
            in_specs=specs,
            out_specs=[gtile, otile],
            out_shape=[jax.ShapeDtypeStruct((heads, tok_dev, head_dim), BF16), grad_shape],
            scratch_shapes=[pltpu.VMEM((width, head_dim, head_dim), F32)] * 2,
            input_output_aliases=aliases,
            compiler_params=pltpu.CompilerParams(dimension_semantics=("arbitrary",)),
        )(*args)
        attended = outs[0]
        axis = 0 if split_out else 2
        grads.append(
            lax.all_to_all(outs[1], ("head", "sub"), split_axis=axis, concat_axis=0, tiled=True)
        )
    if split_out:
        parts = [gr for gr in grads]
    else:
        parts = [gr.reshape(peers, 3, width, tok_out, head_dim) for gr in grads]
    outs = tuple(
        jnp.transpose(
            jnp.stack([p[:, i] for p in parts], 1).reshape(heads * peers, tok_out, head_dim),
            (1, 0, 2),
        )
        for i in range(3)
    )
    return (jnp.transpose(attended, (1, 0, 2)),) + outs


def solution(mesh):
    seq_count = mesh.shape["seq"]
    spec_in = P(("grp", "seq"), ("head", "sub"), None)
    spec_grad = P(("grp", "seq", "head", "sub"), None, None)
    return jax.shard_map(
        lambda *a: per_device(*a, seq_count),
        mesh=mesh,
        in_specs=(spec_in,) * 4,
        out_specs=(spec_in, spec_grad, spec_grad, spec_grad),
        check_vma=False,
    )
```

```python
import functools

import jax
import jax.numpy as jnp
from jax import lax
from jax.experimental import pallas as pl
from jax.experimental.pallas import tpu as pltpu
from jax.sharding import PartitionSpec as P

SPAN = 64
F32 = jnp.float32
BF16 = jnp.bfloat16


def dot_nn(a, b):
    return jnp.dot(a, b, preferred_element_type=F32)


def dot_nt(a, b):
    return lax.dot_general(a, b, (((1,), (1,)), ((), ())), preferred_element_type=F32)


def dot_tn(a, b):
    return lax.dot_general(a, b, (((0,), (0,)), ((), ())), preferred_element_type=F32)


def totals_kernel(heads, q_ref, k_ref, v_ref, d_ref, kv_ref, adj_ref):
    for h in range(heads):
        kv_ref[h] = dot_tn(k_ref[h], v_ref[h])
        adj_ref[h] = dot_tn(d_ref[h], q_ref[h])


def main_kernel(heads, aliased, q_ref, k_ref, v_ref, d_ref, f_ref, before_ref, rest_ref, *refs):
    if aliased:
        refs = refs[1:]
    a_ref, g_ref, state, suffix = refs
    qg_ref, kg_ref, vg_ref = g_ref.at[0], g_ref.at[1], g_ref.at[2]

    @pl.when(pl.program_id(0) == 0)
    def _():
        state[...] = before_ref[...]
        suffix[...] = rest_ref[...]

    factor = f_ref[...]
    span = factor.shape[0]
    row = lax.broadcasted_iota(jnp.int32, (span, span), 0)
    col = lax.broadcasted_iota(jnp.int32, (span, span), 1)
    causal = row >= col
    for h in range(heads):
        qsc = q_ref[h]
        k = k_ref[h]
        v = v_ref[h]
        d = d_ref[h]
        prev = state[h]
        state_low = prev.astype(BF16)
        state[h] = prev + dot_tn(k, v)
        rest = suffix[h] - dot_tn(d, qsc)
        suffix[h] = rest
        suffix_low = rest.astype(BF16)
        scores = jnp.where(causal, dot_nt(qsc, k), 0.0).astype(BF16)
        adj_scores = jnp.where(causal, dot_nt(d, v), 0.0).astype(BF16)
        a_ref[h] = (dot_nn(qsc, state_low) + dot_nn(scores, v)).astype(a_ref.dtype)
        qg_ref[h] = ((dot_nt(d, state_low) + dot_nn(adj_scores, k)) * factor).astype(qg_ref.dtype)
        kg_ref[h] = (dot_nn(v, suffix_low) + dot_tn(adj_scores, qsc)).astype(kg_ref.dtype)
        vg_ref[h] = (dot_nt(k, suffix_low) + dot_tn(scores, d)).astype(vg_ref.dtype)


def exclusive_scan(total, axis, count, reverse):
    carried = jnp.zeros_like(total)
    acc = jnp.zeros_like(total)
    hops = []
    for hop in range(count - 1):
        pair = (count - 1 - hop, count - 2 - hop) if reverse else (hop, hop + 1)
        got = lax.ppermute(carried + total, axis, perm=[pair])
        acc = acc + got
        carried = got
        hops.append(got)
    return acc, hops


def per_device(queries, key_rows, value_rows, out_adjoint, seq_count):
    tok_dev, heads, head_dim = queries.shape
    span = SPAN
    blocks = tok_dev // span
    offset = lax.axis_index("seq") * tok_dev
    position = offset + jnp.arange(tok_dev, dtype=jnp.int32)
    factor = lax.rsqrt(jnp.float32(head_dim) * (position + 1).astype(jnp.float32))[:, None]
    scaled = (queries.astype(F32) * factor[:, :, None]).astype(BF16)
    qh, kh, vh, dh = (jnp.transpose(x, (1, 0, 2)) for x in (scaled, key_rows, value_rows, out_adjoint))

    width = 4 if heads % 4 == 0 and heads > 4 else heads
    groups = heads // width
    state_shape = jax.ShapeDtypeStruct((heads, head_dim, head_dim), F32)
    rows = pl.BlockSpec((width, tok_dev, head_dim), lambda g: (g, 0, 0))
    group_state = pl.BlockSpec((width, head_dim, head_dim), lambda g: (g, 0, 0))
    kv_total, adj_total = pl.pallas_call(
        functools.partial(totals_kernel, width),
        grid=(groups,),
        in_specs=[rows] * 4,
        out_specs=[group_state, group_state],
        out_shape=[state_shape, state_shape],
    )(qh, kh, vh, dh)

    fac = pl.BlockSpec((span, 1), lambda c: (c, 0))
    peers = lax.psum(1, ("head", "sub"))
    tok_out = tok_dev // peers
    split_out = tok_out % span == 0
    per_peer = tok_out // span
    attended = None
    grads = []
    chains = []
    for g in range(groups):
        sel = slice(g * width, (g + 1) * width)
        before, before_hops = exclusive_scan(kv_total[sel], "seq", seq_count, False)
        after, after_hops = exclusive_scan(adj_total[sel], "seq", seq_count, True)
        chains.append([before, after + adj_total[sel], before_hops, after_hops])
    for g in range(groups - 1):
        if seq_count >= 3:
            nxt = chains[g + 1]
            chains[g][0], chains[g][1], _, _ = lax.optimization_barrier(
                (chains[g][0], chains[g][1], nxt[2][seq_count - 3], nxt[3][seq_count - 3])
            )
    for g in range(groups):
        before, rest = chains[g][0], chains[g][1]
        gtile = pl.BlockSpec((width, span, head_dim), lambda c, g=g: (g, c, 0))
        gwhole = pl.BlockSpec((width, head_dim, head_dim), lambda c: (0, 0, 0))
        if split_out:
            otile = pl.BlockSpec(
                (None, 3, width, span, head_dim), lambda c: (c // per_peer, 0, 0, c % per_peer, 0)
            )
            grad_shape = jax.ShapeDtypeStruct((peers, 3, width, tok_out, head_dim), BF16)
        else:
            otile = pl.BlockSpec((3, width, span, head_dim), lambda c: (0, 0, c, 0))
            grad_shape = jax.ShapeDtypeStruct((3, width, tok_dev, head_dim), BF16)
        args = [qh, kh, vh, dh, factor, before, rest]
        specs = [gtile] * 4 + [fac, gwhole, gwhole]
        aliases = {}
        if attended is not None:
            args.append(attended)
            specs.append(pl.BlockSpec(memory_space=pl.ANY))
            aliases = {7: 0}
        outs = pl.pallas_call(
            functools.partial(main_kernel, width, attended is not None),
            grid=(blocks,),
            in_specs=specs,
            out_specs=[gtile, otile],
            out_shape=[jax.ShapeDtypeStruct((heads, tok_dev, head_dim), BF16), grad_shape],
            scratch_shapes=[pltpu.VMEM((width, head_dim, head_dim), F32)] * 2,
            input_output_aliases=aliases,
            compiler_params=pltpu.CompilerParams(dimension_semantics=("arbitrary",)),
        )(*args)
        attended = outs[0]
        axis = 0 if split_out else 2
        grads.append(
            lax.all_to_all(outs[1], ("head", "sub"), split_axis=axis, concat_axis=0, tiled=True)
        )
    if split_out:
        parts = [gr for gr in grads]
    else:
        parts = [gr.reshape(peers, 3, width, tok_out, head_dim) for gr in grads]
    outs = tuple(
        jnp.transpose(
            jnp.stack([p[:, i] for p in parts], 1).reshape(heads * peers, tok_out, head_dim),
            (1, 0, 2),
        )
        for i in range(3)
    )
    return (jnp.transpose(attended, (1, 0, 2)),) + outs


def solution(mesh):
    seq_count = mesh.shape["seq"]
    spec_in = P(("grp", "seq"), ("head", "sub"), None)
    spec_grad = P(("grp", "seq", "head", "sub"), None, None)
    return jax.shard_map(
        lambda *a: per_device(*a, seq_count),
        mesh=mesh,
        in_specs=(spec_in,) * 4,
        out_specs=(spec_in, spec_grad, spec_grad, spec_grad),
        check_vma=False,
    )
```

```python
import functools

import jax
import jax.numpy as jnp
from jax import lax
from jax.experimental import pallas as pl
from jax.experimental.pallas import tpu as pltpu
from jax.sharding import PartitionSpec as P

SPAN = 64
F32 = jnp.float32
BF16 = jnp.bfloat16


def dot_nn(a, b):
    return jnp.dot(a, b, preferred_element_type=F32)


def dot_nt(a, b):
    return lax.dot_general(a, b, (((1,), (1,)), ((), ())), preferred_element_type=F32)


def dot_tn(a, b):
    return lax.dot_general(a, b, (((0,), (0,)), ((), ())), preferred_element_type=F32)


def totals_kernel(heads, q_ref, k_ref, v_ref, d_ref, kv_ref, adj_ref):
    for h in range(heads):
        kv_ref[h] = dot_tn(k_ref[h], v_ref[h])
        adj_ref[h] = dot_tn(d_ref[h], q_ref[h])


def main_kernel(heads, aliased, q_ref, k_ref, v_ref, d_ref, f_ref, before_ref, rest_ref, *refs):
    if aliased:
        refs = refs[1:]
    a_ref, g_ref, state, suffix = refs
    qg_ref, kg_ref, vg_ref = g_ref.at[0], g_ref.at[1], g_ref.at[2]

    @pl.when(pl.program_id(0) == 0)
    def _():
        state[...] = before_ref[...]
        suffix[...] = rest_ref[...]

    factor = f_ref[...]
    span = factor.shape[0]
    row = lax.broadcasted_iota(jnp.int32, (span, span), 0)
    col = lax.broadcasted_iota(jnp.int32, (span, span), 1)
    causal = row >= col
    for h in range(heads):
        qsc = q_ref[h]
        k = k_ref[h]
        v = v_ref[h]
        d = d_ref[h]
        prev = state[h]
        state_low = prev.astype(BF16)
        state[h] = prev + dot_tn(k, v)
        rest = suffix[h] - dot_tn(d, qsc)
        suffix[h] = rest
        suffix_low = rest.astype(BF16)
        scores = jnp.where(causal, dot_nt(qsc, k), 0.0).astype(BF16)
        adj_scores = jnp.where(causal, dot_nt(d, v), 0.0).astype(BF16)
        a_ref[h] = (dot_nn(qsc, state_low) + dot_nn(scores, v)).astype(a_ref.dtype)
        qg_ref[h] = ((dot_nt(d, state_low) + dot_nn(adj_scores, k)) * factor).astype(qg_ref.dtype)
        kg_ref[h] = (dot_nn(v, suffix_low) + dot_tn(adj_scores, qsc)).astype(kg_ref.dtype)
        vg_ref[h] = (dot_nt(k, suffix_low) + dot_tn(scores, d)).astype(vg_ref.dtype)


def exclusive_scan(total, axis, count, reverse):
    carried = jnp.zeros_like(total)
    acc = jnp.zeros_like(total)
    hops = []
    for hop in range(count - 1):
        pair = (count - 1 - hop, count - 2 - hop) if reverse else (hop, hop + 1)
        got = lax.ppermute(carried + total, axis, perm=[pair])
        acc = acc + got
        carried = got
        hops.append(got)
    return acc, hops


def per_device(queries, key_rows, value_rows, out_adjoint, seq_count):
    tok_dev, heads, head_dim = queries.shape
    span = SPAN
    blocks = tok_dev // span
    offset = lax.axis_index("seq") * tok_dev
    position = offset + jnp.arange(tok_dev, dtype=jnp.int32)
    factor = lax.rsqrt(jnp.float32(head_dim) * (position + 1).astype(jnp.float32))[:, None]
    scaled = (queries.astype(F32) * factor[:, :, None]).astype(BF16)
    qh, kh, vh, dh = (jnp.transpose(x, (1, 0, 2)) for x in (scaled, key_rows, value_rows, out_adjoint))

    width = 8 if heads % 8 == 0 and heads > 8 else heads
    groups = heads // width
    state_shape = jax.ShapeDtypeStruct((heads, head_dim, head_dim), F32)
    rows = pl.BlockSpec((width, tok_dev, head_dim), lambda g: (g, 0, 0))
    group_state = pl.BlockSpec((width, head_dim, head_dim), lambda g: (g, 0, 0))
    kv_total, adj_total = pl.pallas_call(
        functools.partial(totals_kernel, width),
        grid=(groups,),
        in_specs=[rows] * 4,
        out_specs=[group_state, group_state],
        out_shape=[state_shape, state_shape],
    )(qh, kh, vh, dh)

    fac = pl.BlockSpec((span, 1), lambda c: (c, 0))
    peers = lax.psum(1, ("head", "sub"))
    tok_out = tok_dev // peers
    split_out = tok_out % span == 0
    per_peer = tok_out // span
    attended = None
    grads = []
    chains = []
    for g in range(groups):
        sel = slice(g * width, (g + 1) * width)
        before, before_hops = exclusive_scan(kv_total[sel], "seq", seq_count, False)
        after, after_hops = exclusive_scan(adj_total[sel], "seq", seq_count, True)
        chains.append([before, after + adj_total[sel], before_hops, after_hops])
    for g in range(groups - 1):
        if seq_count >= 3:
            nxt = chains[g + 1]
            chains[g][0], chains[g][1], _, _ = lax.optimization_barrier(
                (chains[g][0], chains[g][1], nxt[2][seq_count - 3], nxt[3][seq_count - 3])
            )
    for g in range(groups):
        before, rest = chains[g][0], chains[g][1]
        gtile = pl.BlockSpec((width, span, head_dim), lambda c, g=g: (g, c, 0))
        gwhole = pl.BlockSpec((width, head_dim, head_dim), lambda c: (0, 0, 0))
        if split_out:
            otile = pl.BlockSpec(
                (None, 3, width, span, head_dim), lambda c: (c // per_peer, 0, 0, c % per_peer, 0)
            )
            grad_shape = jax.ShapeDtypeStruct((peers, 3, width, tok_out, head_dim), BF16)
        else:
            otile = pl.BlockSpec((3, width, span, head_dim), lambda c: (0, 0, c, 0))
            grad_shape = jax.ShapeDtypeStruct((3, width, tok_dev, head_dim), BF16)
        args = [qh, kh, vh, dh, factor, before, rest]
        specs = [gtile] * 4 + [fac, gwhole, gwhole]
        aliases = {}
        if attended is not None:
            args.append(attended)
            specs.append(pl.BlockSpec(memory_space=pl.ANY))
            aliases = {7: 0}
        outs = pl.pallas_call(
            functools.partial(main_kernel, width, attended is not None),
            grid=(blocks,),
            in_specs=specs,
            out_specs=[gtile, otile],
            out_shape=[jax.ShapeDtypeStruct((heads, tok_dev, head_dim), BF16), grad_shape],
            scratch_shapes=[pltpu.VMEM((width, head_dim, head_dim), F32)] * 2,
            input_output_aliases=aliases,
            compiler_params=pltpu.CompilerParams(dimension_semantics=("arbitrary",)),
        )(*args)
        attended = outs[0]
        sent = outs[1]
        if g + 1 < groups:
            sent, _, _ = lax.optimization_barrier((sent, chains[g + 1][0], chains[g + 1][1]))
        axis = 0 if split_out else 2
        grads.append(
            lax.all_to_all(sent, ("head", "sub"), split_axis=axis, concat_axis=0, tiled=True)
        )
    if split_out:
        parts = [gr for gr in grads]
    else:
        parts = [gr.reshape(peers, 3, width, tok_out, head_dim) for gr in grads]
    outs = tuple(
        jnp.transpose(
            jnp.stack([p[:, i] for p in parts], 1).reshape(heads * peers, tok_out, head_dim),
            (1, 0, 2),
        )
        for i in range(3)
    )
    return (jnp.transpose(attended, (1, 0, 2)),) + outs


def solution(mesh):
    seq_count = mesh.shape["seq"]
    spec_in = P(("grp", "seq"), ("head", "sub"), None)
    spec_grad = P(("grp", "seq", "head", "sub"), None, None)
    return jax.shard_map(
        lambda *a: per_device(*a, seq_count),
        mesh=mesh,
        in_specs=(spec_in,) * 4,
        out_specs=(spec_in, spec_grad, spec_grad, spec_grad),
        check_vma=False,
    )
```

```python
import functools

import jax
import jax.numpy as jnp
from jax import lax
from jax.experimental import pallas as pl
from jax.experimental.pallas import tpu as pltpu
from jax.sharding import PartitionSpec as P

SPAN = 64
F32 = jnp.float32
BF16 = jnp.bfloat16


def dot_nn(a, b):
    return jnp.dot(a, b, preferred_element_type=F32)


def dot_nt(a, b):
    return lax.dot_general(a, b, (((1,), (1,)), ((), ())), preferred_element_type=F32)


def dot_tn(a, b):
    return lax.dot_general(a, b, (((0,), (0,)), ((), ())), preferred_element_type=F32)


def totals_kernel(heads, q_ref, k_ref, v_ref, d_ref, kv_ref, adj_ref):
    for h in range(heads):
        kv_ref[h] = dot_tn(k_ref[h], v_ref[h])
        adj_ref[h] = dot_tn(d_ref[h], q_ref[h])


def main_kernel(heads, aliased, q_ref, k_ref, v_ref, d_ref, f_ref, before_ref, rest_ref, *refs):
    if aliased:
        refs = refs[1:]
    a_ref, g_ref, state, suffix = refs
    qg_ref, kg_ref, vg_ref = g_ref.at[0], g_ref.at[1], g_ref.at[2]

    @pl.when(pl.program_id(0) == 0)
    def _():
        state[...] = before_ref[...]
        suffix[...] = rest_ref[...]

    factor = f_ref[...]
    span = factor.shape[0]
    row = lax.broadcasted_iota(jnp.int32, (span, span), 0)
    col = lax.broadcasted_iota(jnp.int32, (span, span), 1)
    causal = row >= col
    for h in range(heads):
        qsc = q_ref[h]
        k = k_ref[h]
        v = v_ref[h]
        d = d_ref[h]
        prev = state[h]
        state_low = prev.astype(BF16)
        state[h] = prev + dot_tn(k, v)
        rest = suffix[h] - dot_tn(d, qsc)
        suffix[h] = rest
        suffix_low = rest.astype(BF16)
        scores = jnp.where(causal, dot_nt(qsc, k), 0.0).astype(BF16)
        adj_scores = jnp.where(causal, dot_nt(d, v), 0.0).astype(BF16)
        a_ref[h] = (dot_nn(qsc, state_low) + dot_nn(scores, v)).astype(a_ref.dtype)
        qg_ref[h] = ((dot_nt(d, state_low) + dot_nn(adj_scores, k)) * factor).astype(qg_ref.dtype)
        kg_ref[h] = (dot_nn(v, suffix_low) + dot_tn(adj_scores, qsc)).astype(kg_ref.dtype)
        vg_ref[h] = (dot_nt(k, suffix_low) + dot_tn(scores, d)).astype(vg_ref.dtype)


def exclusive_scan(total, axis, count, reverse):
    carried = jnp.zeros_like(total)
    acc = jnp.zeros_like(total)
    hops = []
    for hop in range(count - 1):
        pair = (count - 1 - hop, count - 2 - hop) if reverse else (hop, hop + 1)
        got = lax.ppermute(carried + total, axis, perm=[pair])
        acc = acc + got
        carried = got
        hops.append(got)
    return acc, hops


def per_device(queries, key_rows, value_rows, out_adjoint, seq_count):
    tok_dev, heads, head_dim = queries.shape
    span = SPAN
    blocks = tok_dev // span
    offset = lax.axis_index("seq") * tok_dev
    position = offset + jnp.arange(tok_dev, dtype=jnp.int32)
    factor = lax.rsqrt(jnp.float32(head_dim) * (position + 1).astype(jnp.float32))[:, None]
    scaled = (queries.astype(F32) * factor[:, :, None]).astype(BF16)
    qh, kh, vh, dh = (jnp.transpose(x, (1, 0, 2)) for x in (scaled, key_rows, value_rows, out_adjoint))

    small = heads // 4 if heads % 4 == 0 and heads >= 8 else heads
    starts = [heads - small, 0] if small < heads else [0]
    widths = [small, heads - small] if small < heads else [heads]
    groups = len(widths)
    width = heads // 2 if heads % 16 == 0 else heads
    state_shape = jax.ShapeDtypeStruct((heads, head_dim, head_dim), F32)
    rows = pl.BlockSpec((width, tok_dev, head_dim), lambda g: (g, 0, 0))
    group_state = pl.BlockSpec((width, head_dim, head_dim), lambda g: (g, 0, 0))
    kv_total, adj_total = pl.pallas_call(
        functools.partial(totals_kernel, width),
        grid=(heads // width,),
        in_specs=[rows] * 4,
        out_specs=[group_state, group_state],
        out_shape=[state_shape, state_shape],
    )(qh, kh, vh, dh)

    fac = pl.BlockSpec((span, 1), lambda c: (c, 0))
    peers = lax.psum(1, ("head", "sub"))
    tok_out = tok_dev // peers
    split_out = tok_out % span == 0
    per_peer = tok_out // span
    attended = None
    grads = []
    chains = []
    for g in range(groups):
        sel = slice(starts[g], starts[g] + widths[g])
        before, before_hops = exclusive_scan(kv_total[sel], "seq", seq_count, False)
        after, after_hops = exclusive_scan(adj_total[sel], "seq", seq_count, True)
        chains.append([before, after + adj_total[sel], before_hops, after_hops])
    for g in range(groups - 1):
        if seq_count >= 3:
            nxt = chains[g + 1]
            chains[g][0], chains[g][1], _, _ = lax.optimization_barrier(
                (chains[g][0], chains[g][1], nxt[2][seq_count - 3], nxt[3][seq_count - 3])
            )
    for g in range(groups):
        before, rest = chains[g][0], chains[g][1]
        width = widths[g]
        first = starts[g] // width
        gtile = pl.BlockSpec((width, span, head_dim), lambda c, first=first: (first, c, 0))
        gwhole = pl.BlockSpec((width, head_dim, head_dim), lambda c: (0, 0, 0))
        if split_out:
            otile = pl.BlockSpec(
                (None, 3, width, span, head_dim), lambda c: (c // per_peer, 0, 0, c % per_peer, 0)
            )
            grad_shape = jax.ShapeDtypeStruct((peers, 3, width, tok_out, head_dim), BF16)
        else:
            otile = pl.BlockSpec((3, width, span, head_dim), lambda c: (0, 0, c, 0))
            grad_shape = jax.ShapeDtypeStruct((3, width, tok_dev, head_dim), BF16)
        args = [qh, kh, vh, dh, factor, before, rest]
        specs = [gtile] * 4 + [fac, gwhole, gwhole]
        aliases = {}
        if attended is not None:
            args.append(attended)
            specs.append(pl.BlockSpec(memory_space=pl.ANY))
            aliases = {7: 0}
        outs = pl.pallas_call(
            functools.partial(main_kernel, width, attended is not None),
            grid=(blocks,),
            in_specs=specs,
            out_specs=[gtile, otile],
            out_shape=[jax.ShapeDtypeStruct((heads, tok_dev, head_dim), BF16), grad_shape],
            scratch_shapes=[pltpu.VMEM((width, head_dim, head_dim), F32)] * 2,
            input_output_aliases=aliases,
            compiler_params=pltpu.CompilerParams(dimension_semantics=("arbitrary",)),
        )(*args)
        attended = outs[0]
        axis = 0 if split_out else 2
        grads.append(
            lax.all_to_all(outs[1], ("head", "sub"), split_axis=axis, concat_axis=0, tiled=True)
        )
    if split_out:
        parts = [gr for gr in grads]
    else:
        parts = [gr.reshape(peers, 3, width, tok_out, head_dim) for gr in grads]
    order = sorted(range(groups), key=lambda g: starts[g])
    outs = tuple(
        jnp.transpose(
            jnp.concatenate([parts[g][:, i] for g in order], 1).reshape(heads * peers, tok_out, head_dim),
            (1, 0, 2),
        )
        for i in range(3)
    )
    return (jnp.transpose(attended, (1, 0, 2)),) + outs


def solution(mesh):
    seq_count = mesh.shape["seq"]
    spec_in = P(("grp", "seq"), ("head", "sub"), None)
    spec_grad = P(("grp", "seq", "head", "sub"), None, None)
    return jax.shard_map(
        lambda *a: per_device(*a, seq_count),
        mesh=mesh,
        in_specs=(spec_in,) * 4,
        out_specs=(spec_in, spec_grad, spec_grad, spec_grad),
        check_vma=False,
    )
```

```python
import functools

import jax
import jax.numpy as jnp
from jax import lax
from jax.experimental import pallas as pl
from jax.experimental.pallas import tpu as pltpu
from jax.sharding import PartitionSpec as P

SPAN = 64
F32 = jnp.float32
BF16 = jnp.bfloat16


def dot_nn(a, b):
    return jnp.dot(a, b, preferred_element_type=F32)


def dot_nt(a, b):
    return lax.dot_general(a, b, (((1,), (1,)), ((), ())), preferred_element_type=F32)


def dot_tn(a, b):
    return lax.dot_general(a, b, (((0,), (0,)), ((), ())), preferred_element_type=F32)


def totals_kernel(heads, q_ref, k_ref, v_ref, d_ref, kv_ref, adj_ref):
    for h in range(heads):
        kv_ref[h] = dot_tn(k_ref[h], v_ref[h])
        adj_ref[h] = dot_tn(d_ref[h], q_ref[h])


def main_kernel(heads, aliased, q_ref, k_ref, v_ref, d_ref, f_ref, before_ref, rest_ref, *refs):
    if aliased:
        refs = refs[1:]
    a_ref, g_ref, state, suffix = refs
    qg_ref, kg_ref, vg_ref = g_ref.at[0], g_ref.at[1], g_ref.at[2]

    @pl.when(pl.program_id(0) == 0)
    def _():
        state[...] = before_ref[...]
        suffix[...] = rest_ref[...]

    factor = f_ref[...]
    span = factor.shape[0]
    row = lax.broadcasted_iota(jnp.int32, (span, span), 0)
    col = lax.broadcasted_iota(jnp.int32, (span, span), 1)
    causal = row >= col
    for h in range(heads):
        qsc = q_ref[h]
        k = k_ref[h]
        v = v_ref[h]
        d = d_ref[h]
        prev = state[h]
        state_low = prev.astype(BF16)
        state[h] = prev + dot_tn(k, v)
        rest = suffix[h] - dot_tn(d, qsc)
        suffix[h] = rest
        suffix_low = rest.astype(BF16)
        scores = jnp.where(causal, dot_nt(qsc, k), 0.0).astype(BF16)
        adj_scores = jnp.where(causal, dot_nt(d, v), 0.0).astype(BF16)
        a_ref[h] = (dot_nn(qsc, state_low) + dot_nn(scores, v)).astype(a_ref.dtype)
        qg_ref[h] = ((dot_nt(d, state_low) + dot_nn(adj_scores, k)) * factor).astype(qg_ref.dtype)
        kg_ref[h] = (dot_nn(v, suffix_low) + dot_tn(adj_scores, qsc)).astype(kg_ref.dtype)
        vg_ref[h] = (dot_nt(k, suffix_low) + dot_tn(scores, d)).astype(vg_ref.dtype)


def exclusive_scan(total, axis, count, reverse):
    carried = jnp.zeros_like(total)
    acc = jnp.zeros_like(total)
    hops = []
    for hop in range(count - 1):
        pair = (count - 1 - hop, count - 2 - hop) if reverse else (hop, hop + 1)
        got = lax.ppermute(carried + total, axis, perm=[pair])
        acc = acc + got
        carried = got
        hops.append(got)
    return acc, hops


def per_device(queries, key_rows, value_rows, out_adjoint, seq_count):
    tok_dev, heads, head_dim = queries.shape
    span = SPAN
    blocks = tok_dev // span
    offset = lax.axis_index("seq") * tok_dev
    position = offset + jnp.arange(tok_dev, dtype=jnp.int32)
    factor = lax.rsqrt(jnp.float32(head_dim) * (position + 1).astype(jnp.float32))[:, None]
    scaled = (queries.astype(F32) * factor[:, :, None]).astype(BF16)
    qh, kh, vh, dh = (jnp.transpose(x, (1, 0, 2)) for x in (scaled, key_rows, value_rows, out_adjoint))

    width = 8 if heads % 8 == 0 and heads > 8 else heads
    groups = heads // width
    state_shape = jax.ShapeDtypeStruct((heads, head_dim, head_dim), F32)
    rows = pl.BlockSpec((width, tok_dev, head_dim), lambda g: (g, 0, 0))
    group_state = pl.BlockSpec((width, head_dim, head_dim), lambda g: (g, 0, 0))
    kv_total, adj_total = pl.pallas_call(
        functools.partial(totals_kernel, width),
        grid=(groups,),
        in_specs=[rows] * 4,
        out_specs=[group_state, group_state],
        out_shape=[state_shape, state_shape],
    )(qh, kh, vh, dh)

    fac = pl.BlockSpec((span, 1), lambda c: (c, 0))
    peers = lax.psum(1, ("head", "sub"))
    tok_out = tok_dev // peers
    split_out = tok_out % span == 0
    per_peer = tok_out // span
    attended = None
    grads = []
    chains = []
    for g in range(groups):
        sel = slice(g * width, (g + 1) * width)
        before, before_hops = exclusive_scan(kv_total[sel], "seq", seq_count, False)
        after, after_hops = exclusive_scan(adj_total[sel], "seq", seq_count, True)
        chains.append([before, after + adj_total[sel], before_hops, after_hops])
    for g in range(groups - 1):
        if seq_count >= 3:
            nxt = chains[g + 1]
            chains[g][0], chains[g][1], _, _ = lax.optimization_barrier(
                (chains[g][0], chains[g][1], nxt[2][seq_count - 3], nxt[3][seq_count - 3])
            )
    for g in range(groups):
        before, rest = chains[g][0], chains[g][1]
        gtile = pl.BlockSpec((width, span, head_dim), lambda c, g=g: (g, c, 0))
        gwhole = pl.BlockSpec((width, head_dim, head_dim), lambda c: (0, 0, 0))
        if split_out:
            otile = pl.BlockSpec(
                (None, 3, width, span, head_dim), lambda c: (c // per_peer, 0, 0, c % per_peer, 0)
            )
            grad_shape = jax.ShapeDtypeStruct((peers, 3, width, tok_out, head_dim), BF16)
        else:
            otile = pl.BlockSpec((3, width, span, head_dim), lambda c: (0, 0, c, 0))
            grad_shape = jax.ShapeDtypeStruct((3, width, tok_dev, head_dim), BF16)
        args = [qh, kh, vh, dh, factor, before, rest]
        specs = [gtile] * 4 + [fac, gwhole, gwhole]
        aliases = {}
        if attended is not None:
            args.append(attended)
            specs.append(pl.BlockSpec(memory_space=pl.ANY))
            aliases = {7: 0}
        outs = pl.pallas_call(
            functools.partial(main_kernel, width, attended is not None),
            grid=(blocks,),
            in_specs=specs,
            out_specs=[gtile, otile],
            out_shape=[jax.ShapeDtypeStruct((heads, tok_dev, head_dim), BF16), grad_shape],
            scratch_shapes=[pltpu.VMEM((width, head_dim, head_dim), F32)] * 2,
            input_output_aliases=aliases,
            compiler_params=pltpu.CompilerParams(dimension_semantics=("arbitrary",)),
            cost_estimate=pl.CostEstimate(
                flops=360 * width * tok_dev * span * head_dim * head_dim // span,
                transcendentals=0,
                bytes_accessed=16 * width * tok_dev * head_dim,
            ),
        )(*args)
        attended = outs[0]
        axis = 0 if split_out else 2
        grads.append(
            lax.all_to_all(outs[1], ("head", "sub"), split_axis=axis, concat_axis=0, tiled=True)
        )
    if split_out:
        parts = [gr for gr in grads]
    else:
        parts = [gr.reshape(peers, 3, width, tok_out, head_dim) for gr in grads]
    outs = tuple(
        jnp.transpose(
            jnp.stack([p[:, i] for p in parts], 1).reshape(heads * peers, tok_out, head_dim),
            (1, 0, 2),
        )
        for i in range(3)
    )
    return (jnp.transpose(attended, (1, 0, 2)),) + outs


def solution(mesh):
    seq_count = mesh.shape["seq"]
    spec_in = P(("grp", "seq"), ("head", "sub"), None)
    spec_grad = P(("grp", "seq", "head", "sub"), None, None)
    return jax.shard_map(
        lambda *a: per_device(*a, seq_count),
        mesh=mesh,
        in_specs=(spec_in,) * 4,
        out_specs=(spec_in, spec_grad, spec_grad, spec_grad),
        check_vma=False,
    )
```

```python
import functools

import jax
import jax.numpy as jnp
from jax import lax
from jax.experimental import pallas as pl
from jax.experimental.pallas import tpu as pltpu
from jax.sharding import PartitionSpec as P

SPAN = 64
F32 = jnp.float32
BF16 = jnp.bfloat16


def dot_nn(a, b):
    return jnp.dot(a, b, preferred_element_type=F32)


def dot_nt(a, b):
    return lax.dot_general(a, b, (((1,), (1,)), ((), ())), preferred_element_type=F32)


def dot_tn(a, b):
    return lax.dot_general(a, b, (((0,), (0,)), ((), ())), preferred_element_type=F32)


def totals_kernel(heads, q_ref, k_ref, v_ref, d_ref, kv_ref, adj_ref):
    for h in range(heads):
        kv_ref[h] = dot_tn(k_ref[h], v_ref[h])
        adj_ref[h] = dot_tn(d_ref[h], q_ref[h])


def main_kernel(heads, aliased, q_ref, k_ref, v_ref, d_ref, f_ref, before_ref, rest_ref, *refs):
    if aliased:
        refs = refs[1:]
    a_ref, g_ref, state, suffix = refs
    qg_ref, kg_ref, vg_ref = g_ref.at[0], g_ref.at[1], g_ref.at[2]

    @pl.when(pl.program_id(0) == 0)
    def _():
        state[...] = before_ref[...]
        suffix[...] = rest_ref[...]

    factor = f_ref[...]
    span = factor.shape[0]
    row = lax.broadcasted_iota(jnp.int32, (span, span), 0)
    col = lax.broadcasted_iota(jnp.int32, (span, span), 1)
    causal = row >= col
    for h in range(heads):
        qsc = q_ref[h]
        k = k_ref[h]
        v = v_ref[h]
        d = d_ref[h]
        prev = state[h]
        state_low = prev.astype(BF16)
        state[h] = prev + dot_tn(k, v)
        rest = suffix[h] - dot_tn(d, qsc)
        suffix[h] = rest
        suffix_low = rest.astype(BF16)
        scores = jnp.where(causal, dot_nt(qsc, k), 0.0).astype(BF16)
        adj_scores = jnp.where(causal, dot_nt(d, v), 0.0).astype(BF16)
        a_ref[h] = (dot_nn(qsc, state_low) + dot_nn(scores, v)).astype(a_ref.dtype)
        qg_ref[h] = ((dot_nt(d, state_low) + dot_nn(adj_scores, k)) * factor).astype(qg_ref.dtype)
        kg_ref[h] = (dot_nn(v, suffix_low) + dot_tn(adj_scores, qsc)).astype(kg_ref.dtype)
        vg_ref[h] = (dot_nt(k, suffix_low) + dot_tn(scores, d)).astype(vg_ref.dtype)


def exclusive_scan(total, axis, count, reverse):
    carried = jnp.zeros_like(total)
    acc = jnp.zeros_like(total)
    hops = []
    for hop in range(count - 1):
        pair = (count - 1 - hop, count - 2 - hop) if reverse else (hop, hop + 1)
        got = lax.ppermute(carried + total, axis, perm=[pair])
        acc = acc + got
        carried = got
        hops.append(got)
    return acc, hops


def per_device(queries, key_rows, value_rows, out_adjoint, seq_count):
    tok_dev, heads, head_dim = queries.shape
    span = SPAN
    blocks = tok_dev // span
    offset = lax.axis_index("seq") * tok_dev
    position = offset + jnp.arange(tok_dev, dtype=jnp.int32)
    factor = lax.rsqrt(jnp.float32(head_dim) * (position + 1).astype(jnp.float32))[:, None]
    scaled = (queries.astype(F32) * factor[:, :, None]).astype(BF16)
    qh, kh, vh, dh = (jnp.transpose(x, (1, 0, 2)) for x in (scaled, key_rows, value_rows, out_adjoint))

    small = heads // 4 if heads % 4 == 0 and heads >= 8 else heads
    starts = [heads - small, 0] if small < heads else [0]
    widths = [small, heads - small] if small < heads else [heads]
    groups = len(widths)
    width = heads // 2 if heads % 16 == 0 else heads
    state_shape = jax.ShapeDtypeStruct((heads, head_dim, head_dim), F32)
    rows = pl.BlockSpec((width, tok_dev, head_dim), lambda g: (g, 0, 0))
    group_state = pl.BlockSpec((width, head_dim, head_dim), lambda g: (g, 0, 0))
    kv_total, adj_total = pl.pallas_call(
        functools.partial(totals_kernel, width),
        grid=(heads // width,),
        in_specs=[rows] * 4,
        out_specs=[group_state, group_state],
        out_shape=[state_shape, state_shape],
    )(qh, kh, vh, dh)

    fac = pl.BlockSpec((span, 1), lambda c: (c, 0))
    peers = lax.psum(1, ("head", "sub"))
    tok_out = tok_dev // peers
    split_out = tok_out % span == 0
    per_peer = tok_out // span
    attended = None
    grads = []
    chains = []
    for g in range(groups):
        sel = slice(starts[g], starts[g] + widths[g])
        before, before_hops = exclusive_scan(kv_total[sel], "seq", seq_count, False)
        after, after_hops = exclusive_scan(adj_total[sel], "seq", seq_count, True)
        chains.append([before, after + adj_total[sel], before_hops, after_hops])
    for g in range(groups - 1):
        if seq_count >= 3:
            nxt = chains[g + 1]
            chains[g][0], chains[g][1], _, _ = lax.optimization_barrier(
                (chains[g][0], chains[g][1], nxt[2][seq_count - 3], nxt[3][seq_count - 3])
            )
    for g in range(groups):
        before, rest = chains[g][0], chains[g][1]
        width = widths[g]
        first = starts[g] // width
        gtile = pl.BlockSpec((width, span, head_dim), lambda c, first=first: (first, c, 0))
        gwhole = pl.BlockSpec((width, head_dim, head_dim), lambda c: (0, 0, 0))
        if split_out:
            otile = pl.BlockSpec(
                (None, 3, width, span, head_dim), lambda c: (c // per_peer, 0, 0, c % per_peer, 0)
            )
            grad_shape = jax.ShapeDtypeStruct((peers, 3, width, tok_out, head_dim), BF16)
        else:
            otile = pl.BlockSpec((3, width, span, head_dim), lambda c: (0, 0, c, 0))
            grad_shape = jax.ShapeDtypeStruct((3, width, tok_dev, head_dim), BF16)
        args = [qh, kh, vh, dh, factor, before, rest]
        specs = [gtile] * 4 + [fac, gwhole, gwhole]
        aliases = {}
        if attended is not None:
            args.append(attended)
            specs.append(pl.BlockSpec(memory_space=pl.ANY))
            aliases = {7: 0}
        outs = pl.pallas_call(
            functools.partial(main_kernel, width, attended is not None),
            grid=(blocks,),
            in_specs=specs,
            out_specs=[gtile, otile],
            out_shape=[jax.ShapeDtypeStruct((heads, tok_dev, head_dim), BF16), grad_shape],
            scratch_shapes=[pltpu.VMEM((width, head_dim, head_dim), F32)] * 2,
            input_output_aliases=aliases,
            compiler_params=pltpu.CompilerParams(dimension_semantics=("arbitrary",)),
            cost_estimate=pl.CostEstimate(
                flops=360 * width * tok_dev * span * head_dim * head_dim // span,
                transcendentals=0,
                bytes_accessed=16 * width * tok_dev * head_dim,
            ),
        )(*args)
        attended = outs[0]
        axis = 0 if split_out else 2
        grads.append(
            lax.all_to_all(outs[1], ("head", "sub"), split_axis=axis, concat_axis=0, tiled=True)
        )
    if split_out:
        parts = [gr for gr in grads]
    else:
        parts = [gr.reshape(peers, 3, width, tok_out, head_dim) for gr in grads]
    order = sorted(range(groups), key=lambda g: starts[g])
    outs = tuple(
        jnp.transpose(
            jnp.concatenate([parts[g][:, i] for g in order], 1).reshape(heads * peers, tok_out, head_dim),
            (1, 0, 2),
        )
        for i in range(3)
    )
    return (jnp.transpose(attended, (1, 0, 2)),) + outs


def solution(mesh):
    seq_count = mesh.shape["seq"]
    spec_in = P(("grp", "seq"), ("head", "sub"), None)
    spec_grad = P(("grp", "seq", "head", "sub"), None, None)
    return jax.shard_map(
        lambda *a: per_device(*a, seq_count),
        mesh=mesh,
        in_specs=(spec_in,) * 4,
        out_specs=(spec_in, spec_grad, spec_grad, spec_grad),
        check_vma=False,
    )
```
